32 devices in a mesh: grp: 2 (over y), seq: 4 (over z), head: 2 (over x), rep: 2 (over core).
Axes of the slice: x: 2, y: 2, z: 4, core: 2. Of those that a mesh axis runs over, the one named last changes fastest.
Arguments:
- query: bfloat16 [8192, 1280], P(('grp', 'seq', 'rep'), 'head'), parts along dimension 0, may hold values from -22 to 22
- key_value: bfloat16 [2, 8192, 1280], P(None, ('grp', 'seq'), 'head'), parts along dimension 1, may hold values from -6 to 6
- key_blocks: int32 [64, 8], P(('grp', 'seq', 'rep')), parts along dimension 0, may hold values from -1 to 31, as said below
Outputs:
- attended: bfloat16 [8192, 1280], P(('grp', 'seq', 'rep'), 'head'), parts along dimension 0
The draws below stay inside these ranges and needn't reach their ends.
There are 2 independent parts, one for each index of `grp`. The reference program is written for one: setup_inputs(seed, part) draws one part's arguments, and reference() takes and returns one part's arrays. A program takes and returns all parts, laid end to end along the dimension named above; each array names one. Nothing has to cross between parts.
Inputs may be any that keep to these rules, and one draw needn't show every extreme that they name: `key_blocks`: slab q holds blocks q * 8 to (q + 1) * 8 - 1. Entry j = 2 * k + s (k < 4, s in 0, 1) of the row of a query block of slab q names one block of slab p = q + (1 - 2 * s) * 2^(k + 1) if 0 <= p < 4, and is -1 otherwise. The blocks named in column j by all rows of slab q are p * 8 + phase + 4 * c with c in 0 to 1 and one phase in 0 to 3 common to all rows of slab q in that column.
All inputs are finite; a program needn't handle non-finite values.
Results may differ from the reference program's by a relative error of at most 0.0049.
Values may be sent and summed in bfloat16 or wider, within the bound.
No kernel may reach another device: no remote copies, remote signals or barrier semaphores. Data moves between devices by JAX's collectives and lax.ppermute only.
A program may use at most 64 MiB of HBM per device.

```python
import math
import jax
import jax.numpy as jnp
from jax import lax

HEAD_WIDTH = 128
MASK_BLOCK_SIZE = 128
BLOCKS_PER_FRAME = 4
FAR_STRIDE = 4
LEVELS = 4
HEAD_TOTAL = 10
SLAB_BLK = 8
FAR_SLOT_COUNT = 8
QBLOCKS = 32
TOKENS = 4096


def draw_query(key, part):
    columns = HEAD_TOTAL * HEAD_WIDTH
    own_key = jax.random.fold_in(key, 21)
    values = jnp.clip(2.0 * jax.random.normal(own_key, (TOKENS, columns), jnp.float32), -12.0, 12.0)
    return values.astype(jnp.bfloat16)


def draw_key_value(key, part):
    columns = HEAD_TOTAL * HEAD_WIDTH
    own_key = jax.random.fold_in(key, 33)
    first_key = jax.random.fold_in(own_key, 0)
    values = jnp.clip(jax.random.normal(first_key, (2, TOKENS, columns), jnp.float32), -6.0, 6.0)
    return values.astype(jnp.bfloat16)


def draw_key_blocks(key, part):
    slab_count = QBLOCKS // SLAB_BLK
    far_count = SLAB_BLK // FAR_STRIDE
    phase_key, pick_key = jax.random.split(jax.random.fold_in(key, 11))
    phases = jax.random.randint(phase_key, (slab_count, 2 * LEVELS), 0, FAR_STRIDE)
    picks = jax.random.randint(pick_key, (QBLOCKS, 2 * LEVELS), 0, far_count)
    slab_of = jnp.arange(QBLOCKS, dtype=jnp.int32) // SLAB_BLK
    tiers = jnp.arange(2 * LEVELS, dtype=jnp.int32) // 2
    sides = jnp.arange(2 * LEVELS, dtype=jnp.int32) % 2
    offsets = (1 - 2 * sides) * jnp.left_shift(jnp.int32(2), tiers)
    partner = slab_of[:, None] + offsets[None, :]
    block_ids = partner * SLAB_BLK + phases[slab_of] + FAR_STRIDE * picks
    inside = (partner >= 0) & (partner < slab_count)
    return jnp.where(inside, block_ids, -1).astype(jnp.int32)


def setup_inputs(seed: int = 0, part: int = 0) -> dict:
    arg_keys = jax.random.split(jax.random.key(seed), 4)
    own_keys = jax.random.split(jax.random.fold_in(arg_keys[3], part), 4)
    query = draw_query(jax.random.fold_in(jax.random.fold_in(arg_keys[3], part), 71), part)
    key_value = draw_key_value(jax.random.fold_in(jax.random.fold_in(arg_keys[3], part), 71), part)
    key_blocks = draw_key_blocks(jax.random.fold_in(jax.random.fold_in(arg_keys[3], part), 71), part)
    return {"query": query, "key_value": key_value, "key_blocks": key_blocks}


def reference(query, key_value, key_blocks):
    frame_rows = BLOCKS_PER_FRAME * MASK_BLOCK_SIZE
    all_frames = TOKENS // frame_rows
    columns = HEAD_TOTAL * HEAD_WIDTH
    score_scale = 1.0 / math.sqrt(HEAD_WIDTH)
    padded = jnp.pad(key_value, ((0, 0), (frame_rows, frame_rows), (0, 0)))
    block_table = key_value.reshape(2, QBLOCKS, MASK_BLOCK_SIZE, columns)

    def one_frame(frame_index):
        first_row = frame_index * frame_rows
        query_rows = lax.dynamic_slice_in_dim(query, first_row, frame_rows, 0)
        query_rows = query_rows.astype(jnp.float32).reshape(BLOCKS_PER_FRAME, MASK_BLOCK_SIZE, HEAD_TOTAL, HEAD_WIDTH)
        near_pair = lax.dynamic_slice_in_dim(padded, first_row, 3 * frame_rows, 1)
        near_pair = near_pair.astype(jnp.float32).reshape(2, 3 * frame_rows, HEAD_TOTAL, HEAD_WIDTH)
        near_frame = frame_index - 1 + jnp.arange(3 * frame_rows, dtype=jnp.int32) // frame_rows
        near_valid = (near_frame >= 0) & (near_frame < all_frames)
        block_ids = lax.dynamic_slice_in_dim(key_blocks, frame_index * BLOCKS_PER_FRAME, BLOCKS_PER_FRAME, 0)
        far_key_pairing = block_table[:, jnp.maximum(block_ids, 0)]
        far_key_pairing = far_key_pairing.astype(jnp.float32).reshape(2, BLOCKS_PER_FRAME, FAR_SLOT_COUNT * MASK_BLOCK_SIZE, HEAD_TOTAL, HEAD_WIDTH)
        far_valid = jnp.repeat(block_ids >= 0, MASK_BLOCK_SIZE, axis=1)
        near_scores = jnp.einsum('bqhd,khd->hbqk', query_rows, near_pair[0]) * score_scale
        near_scores = jnp.where(near_valid[None, None, None, :], near_scores, -jnp.inf)
        far_scores = jnp.einsum('bqhd,bkhd->hbqk', query_rows, far_key_pairing[0]) * score_scale
        far_scores = jnp.where(far_valid[None, :, None, :], far_scores, -jnp.inf)
        row_top = jnp.maximum(lax.optimization_barrier(jnp.max(near_scores, axis=3)), lax.optimization_barrier(jnp.max(far_scores, axis=3)))[..., None]
        near_exp = jnp.exp(near_scores - row_top)
        far_exp = jnp.exp(far_scores - row_top)
        row_total = lax.optimization_barrier(jnp.sum(near_exp, axis=3, keepdims=True)) + lax.optimization_barrier(jnp.sum(far_exp, axis=3, keepdims=True))
        near_prob = lax.optimization_barrier((near_exp / row_total).astype(jnp.bfloat16)).astype(jnp.float32)
        far_probability = lax.optimization_barrier((far_exp / row_total).astype(jnp.bfloat16)).astype(jnp.float32)
        mixed = jnp.einsum('hbqk,khd->bqhd', near_prob, near_pair[1])
        mixed = mixed + jnp.einsum('hbqk,bkhd->bqhd', far_probability, far_key_pairing[1])
        return mixed.reshape(frame_rows, columns).astype(jnp.bfloat16)
    outputs = lax.map(one_frame, jnp.arange(all_frames, dtype=jnp.int32))
    return outputs.reshape(TOKENS, columns)
```

```python
import math

import jax
import jax.numpy as jnp
from jax import lax
from jax.sharding import PartitionSpec as P

HEAD_WIDTH = 128
MASK_BLOCK_SIZE = 128
BLOCKS_PER_FRAME = 4
FAR_STRIDE = 4
LEVELS = 4


def from_behind(shard, axis, by):
    count = lax.axis_size(axis)
    pairs = [(i, i + by) for i in range(count) if 0 <= i + by < count]
    return lax.ppermute(shard, axis, pairs)


def halo_frame(key_value, frame_rows, seq_count, rep_count, rep_index):
    slab_rows = key_value.shape[1]
    start = jnp.where(rep_index == rep_count - 1, slab_rows - frame_rows, 0)
    payload = lax.dynamic_slice_in_dim(key_value, start, frame_rows, 1)
    pairs = []
    for s in range(seq_count - 1):
        pairs.append((s * rep_count + rep_count - 1, (s + 1) * rep_count))
    for s in range(1, seq_count):
        pairs.append((s * rep_count, (s - 1) * rep_count + rep_count - 1))
    return lax.ppermute(payload, ("seq", "rep"), pairs)


def per_device(query, key_value, key_blocks):
    frame_rows = BLOCKS_PER_FRAME * MASK_BLOCK_SIZE
    query_count = query.shape[0]
    slab_rows = key_value.shape[1]
    columns = key_value.shape[2]
    head_count = columns // HEAD_WIDTH
    slab_blocks = slab_rows // MASK_BLOCK_SIZE
    slab_frames = slab_rows // frame_rows
    far_count = slab_blocks // FAR_STRIDE
    seq_count = lax.axis_size("seq")
    rep_count = lax.axis_size("rep")
    slab_index = lax.axis_index("seq")
    rep_index = lax.axis_index("rep")
    query_frames = query_count // frame_rows
    query_blocks = query_count // MASK_BLOCK_SIZE
    score_scale = 1.0 / math.sqrt(HEAD_WIDTH)
    assert rep_count >= 2 and query_frames * rep_count == slab_frames
    assert far_count % rep_count == 0
    far_share = far_count // rep_count

    halo = halo_frame(key_value, frame_rows, seq_count, rep_count, rep_index)

    phases = jnp.maximum(key_blocks[0], 0) % FAR_STRIDE
    stride_grid = key_value.reshape(2, far_count, FAR_STRIDE, MASK_BLOCK_SIZE, columns)
    share_grid = lax.dynamic_slice_in_dim(stride_grid, rep_index * far_share, far_share, 1)
    received = []
    pick_list = []
    valid_list = []
    for tier_index in range(LEVELS):
        distance = 2 ** (tier_index + 1)
        if distance < seq_count:
            for direction in range(2):
                slot_index = 2 * tier_index + direction
                offset = (1 - 2 * direction) * distance
                wanted = from_behind(phases[slot_index : slot_index + 1], "seq", offset)[0]
                chosen = lax.dynamic_index_in_dim(share_grid, wanted, 2, keepdims=False)
                received.append(from_behind(chosen, "seq", -offset))
                partner = slab_index + offset
                inside = (partner >= 0) & (partner < seq_count)
                named = key_blocks[:, slot_index]
                pick = (named - partner * slab_blocks - phases[slot_index]) // FAR_STRIDE
                pick_list.append(pick)
                valid_list.append((named >= 0) & inside)
    slot_count = len(received)
    mine = jnp.stack(received, 1)
    parts = [mine]
    sources = [rep_index]
    for k in range(1, rep_count):
        shift = [(r, (r + k) % rep_count) for r in range(rep_count)]
        parts.append(lax.ppermute(mine, "rep", shift))
        sources.append((rep_index - k) % rep_count)
    far_pair = jnp.stack(parts, 2).reshape(2, slot_count * far_count * MASK_BLOCK_SIZE, columns)
    far_pick = jnp.stack(pick_list, 1)
    far_valid = jnp.stack(valid_list, 1)
    share_ids = jnp.arange(far_share, dtype=jnp.int32)
    candidates = (jnp.stack(sources)[:, None] * far_share + share_ids[None, :]).reshape(far_count)
    far_mask = far_valid[:, :, None] & (far_pick[:, :, None] == candidates[None, None, :])
    far_mask = jnp.repeat(far_mask.reshape(query_blocks, slot_count * far_count), MASK_BLOCK_SIZE, axis=1)
    far_mask = jnp.repeat(far_mask, MASK_BLOCK_SIZE, axis=0)

    query_heads = query.reshape(query_count, head_count, HEAD_WIDTH)
    own_pair = key_value.reshape(2, slab_rows, head_count, HEAD_WIDTH)

    own_scores = (
        jnp.einsum("qhd,khd->hqk", query_heads, own_pair[0], preferred_element_type=jnp.float32)
        * score_scale
    )
    own_top = jnp.max(own_scores, axis=2, keepdims=True)
    own_exp = jnp.exp(own_scores - own_top)
    own_total = jnp.sum(own_exp, axis=2, keepdims=True)

    halo_pair = halo.reshape(2, frame_rows, head_count, HEAD_WIDTH)
    far_heads = far_pair.reshape(2, far_pair.shape[1], head_count, HEAD_WIDTH)
    halo_valid = ((rep_index == 0) & (slab_index > 0)) | (
        (rep_index == rep_count - 1) & (slab_index < seq_count - 1)
    )
    halo_scores = (
        jnp.einsum("qhd,khd->hqk", query_heads, halo_pair[0], preferred_element_type=jnp.float32)
        * score_scale
    )
    halo_scores = jnp.where(halo_valid, halo_scores, -jnp.inf)
    far_scores = (
        jnp.einsum("qhd,khd->hqk", query_heads, far_heads[0], preferred_element_type=jnp.float32)
        * score_scale
    )
    far_scores = jnp.where(far_mask[None], far_scores, -jnp.inf)
    row_top = jnp.maximum(
        own_top,
        jnp.maximum(
            jnp.max(halo_scores, axis=2, keepdims=True), jnp.max(far_scores, axis=2, keepdims=True)
        ),
    )
    own_factor = jnp.exp(own_top - row_top)
    halo_exp = jnp.exp(halo_scores - row_top)
    far_exp = jnp.exp(far_scores - row_top)
    row_total = (
        own_total * own_factor
        + jnp.sum(halo_exp, axis=2, keepdims=True)
        + jnp.sum(far_exp, axis=2, keepdims=True)
    )
    own_prob = (own_exp * (own_factor / row_total)).astype(jnp.bfloat16)
    halo_prob = (halo_exp / row_total).astype(jnp.bfloat16)
    far_prob = (far_exp / row_total).astype(jnp.bfloat16)
    mixed = jnp.einsum("hqk,khd->qhd", own_prob, own_pair[1], preferred_element_type=jnp.float32)
    mixed = mixed + jnp.einsum(
        "hqk,khd->qhd", halo_prob, halo_pair[1], preferred_element_type=jnp.float32
    )
    mixed = mixed + jnp.einsum(
        "hqk,khd->qhd", far_prob, far_heads[1], preferred_element_type=jnp.float32
    )
    return mixed.reshape(query_count, columns).astype(jnp.bfloat16)


def solution(mesh):
    in_specs = (
        P(("grp", "seq", "rep"), "head"),
        P(None, ("grp", "seq"), "head"),
        P(("grp", "seq", "rep"), None),
    )
    out_specs = P(("grp", "seq", "rep"), "head")
    return jax.shard_map(
        per_device, mesh=mesh, in_specs=in_specs, out_specs=out_specs, check_vma=False
    )
```

```python
import math

import jax
import jax.numpy as jnp
from jax import lax
from jax.sharding import PartitionSpec as P

HEAD_WIDTH = 128
MASK_BLOCK_SIZE = 128
BLOCKS_PER_FRAME = 4
FAR_STRIDE = 4
LEVELS = 4


def from_behind(shard, axis, by):
    count = lax.axis_size(axis)
    pairs = [(i, i + by) for i in range(count) if 0 <= i + by < count]
    return lax.ppermute(shard, axis, pairs)


def halo_frame(key_value, frame_rows, seq_count, rep_count, rep_index):
    slab_rows = key_value.shape[1]
    last = lax.slice_in_dim(key_value, slab_rows - frame_rows, slab_rows, axis=1)
    first = lax.slice_in_dim(key_value, 0, frame_rows, axis=1)
    forward = [(s * rep_count + rep_count - 1, (s + 1) * rep_count) for s in range(seq_count - 1)]
    backward = [(s * rep_count, (s - 1) * rep_count + rep_count - 1) for s in range(1, seq_count)]
    low = lax.ppermute(last, ("seq", "rep"), forward)
    high = lax.ppermute(first, ("seq", "rep"), backward)
    return jnp.where(rep_index == 0, low, high)


def per_device(query, key_value, key_blocks):
    frame_rows = BLOCKS_PER_FRAME * MASK_BLOCK_SIZE
    query_count = query.shape[0]
    slab_rows = key_value.shape[1]
    columns = key_value.shape[2]
    head_count = columns // HEAD_WIDTH
    slab_blocks = slab_rows // MASK_BLOCK_SIZE
    slab_frames = slab_rows // frame_rows
    far_count = slab_blocks // FAR_STRIDE
    seq_count = lax.axis_size("seq")
    rep_count = lax.axis_size("rep")
    slab_index = lax.axis_index("seq")
    rep_index = lax.axis_index("rep")
    query_frames = query_count // frame_rows
    query_blocks = query_count // MASK_BLOCK_SIZE
    score_scale = 1.0 / math.sqrt(HEAD_WIDTH)
    assert rep_count >= 2 and query_frames * rep_count == slab_frames
    assert far_count % rep_count == 0
    far_share = far_count // rep_count

    halo = halo_frame(key_value, frame_rows, seq_count, rep_count, rep_index)

    phases = jnp.maximum(key_blocks[0], 0) % FAR_STRIDE
    stride_grid = key_value.reshape(2, far_count, FAR_STRIDE, MASK_BLOCK_SIZE, columns)
    share_grid = lax.dynamic_slice_in_dim(stride_grid, rep_index * far_share, far_share, 1)
    received = []
    pick_list = []
    valid_list = []
    for tier_index in range(LEVELS):
        distance = 2 ** (tier_index + 1)
        if distance < seq_count:
            for direction in range(2):
                slot_index = 2 * tier_index + direction
                offset = (1 - 2 * direction) * distance
                wanted = from_behind(phases[slot_index : slot_index + 1], "seq", offset)[0]
                chosen = lax.dynamic_index_in_dim(share_grid, wanted, 2, keepdims=False)
                received.append((chosen, -offset))
                partner = slab_index + offset
                inside = (partner >= 0) & (partner < seq_count)
                named = key_blocks[:, slot_index]
                pick = (named - partner * slab_blocks - phases[slot_index]) // FAR_STRIDE
                pick_list.append(pick)
                valid_list.append((named >= 0) & inside)
    query, payloads = lax.optimization_barrier((query, [chosen for chosen, _ in received]))
    received = [from_behind(chosen, "seq", by) for chosen, (_, by) in zip(payloads, received)]
    slot_count = len(received)
    mine = jnp.stack(received, 1)
    parts = [mine]
    sources = [rep_index]
    for k in range(1, rep_count):
        shift = [(r, (r + k) % rep_count) for r in range(rep_count)]
        parts.append(lax.ppermute(mine, "rep", shift))
        sources.append((rep_index - k) % rep_count)
    far_pair = jnp.stack(parts, 2).reshape(2, slot_count * far_count * MASK_BLOCK_SIZE, columns)
    far_pick = jnp.stack(pick_list, 1)
    far_valid = jnp.stack(valid_list, 1)
    share_ids = jnp.arange(far_share, dtype=jnp.int32)
    candidates = (jnp.stack(sources)[:, None] * far_share + share_ids[None, :]).reshape(far_count)
    far_mask = far_valid[:, :, None] & (far_pick[:, :, None] == candidates[None, None, :])
    far_mask = jnp.repeat(far_mask.reshape(query_blocks, slot_count * far_count), MASK_BLOCK_SIZE, axis=1)
    far_mask = jnp.repeat(far_mask, MASK_BLOCK_SIZE, axis=0)

    halo_valid = ((rep_index == 0) & (slab_index > 0)) | (
        (rep_index == rep_count - 1) & (slab_index < seq_count - 1)
    )
    outputs = []
    for head in range(head_count):
        cols = slice(head * HEAD_WIDTH, (head + 1) * HEAD_WIDTH)
        query_head = query[:, cols]
        own_scores = (
            jnp.dot(query_head, key_value[0, :, cols].T, preferred_element_type=jnp.float32)
            * score_scale
        )
        own_top = jnp.max(own_scores, axis=1, keepdims=True)
        own_exp = jnp.exp(own_scores - own_top)
        own_total = jnp.sum(own_exp, axis=1, keepdims=True)
        halo_scores = (
            jnp.dot(query_head, halo[0, :, cols].T, preferred_element_type=jnp.float32)
            * score_scale
        )
        halo_scores = jnp.where(halo_valid, halo_scores, -jnp.inf)
        far_scores = (
            jnp.dot(query_head, far_pair[0, :, cols].T, preferred_element_type=jnp.float32)
            * score_scale
        )
        far_scores = jnp.where(far_mask, far_scores, -jnp.inf)
        row_top = jnp.maximum(
            own_top,
            jnp.maximum(
                jnp.max(halo_scores, axis=1, keepdims=True),
                jnp.max(far_scores, axis=1, keepdims=True),
            ),
        )
        own_factor = jnp.exp(own_top - row_top)
        halo_exp = jnp.exp(halo_scores - row_top)
        far_exp = jnp.exp(far_scores - row_top)
        row_total = (
            own_total * own_factor
            + jnp.sum(halo_exp, axis=1, keepdims=True)
            + jnp.sum(far_exp, axis=1, keepdims=True)
        )
        own_prob = (own_exp * (own_factor / row_total)).astype(jnp.bfloat16)
        halo_prob = (halo_exp / row_total).astype(jnp.bfloat16)
        far_prob = (far_exp / row_total).astype(jnp.bfloat16)
        mixed = jnp.dot(own_prob, key_value[1, :, cols], preferred_element_type=jnp.float32)
        mixed = mixed + jnp.dot(halo_prob, halo[1, :, cols], preferred_element_type=jnp.float32)
        mixed = mixed + jnp.dot(far_prob, far_pair[1, :, cols], preferred_element_type=jnp.float32)
        outputs.append(mixed.astype(jnp.bfloat16))
    return jnp.concatenate(outputs, axis=1)


def solution(mesh):
    in_specs = (
        P(("grp", "seq", "rep"), "head"),
        P(None, ("grp", "seq"), "head"),
        P(("grp", "seq", "rep"), None),
    )
    out_specs = P(("grp", "seq", "rep"), "head")
    return jax.shard_map(
        per_device, mesh=mesh, in_specs=in_specs, out_specs=out_specs, check_vma=False
    )
```

```python
import math

import jax
import jax.numpy as jnp
from jax import lax
from jax.sharding import PartitionSpec as P

HEAD_WIDTH = 128
MASK_BLOCK_SIZE = 128
BLOCKS_PER_FRAME = 4
FAR_STRIDE = 4
LEVELS = 4


def from_behind(shard, axis, by):
    count = lax.axis_size(axis)
    pairs = [(i, i + by) for i in range(count) if 0 <= i + by < count]
    return lax.ppermute(shard, axis, pairs)


def halo_frame(key_value, frame_rows, seq_count, rep_count, rep_index):
    slab_rows = key_value.shape[1]
    last = lax.slice_in_dim(key_value, slab_rows - frame_rows, slab_rows, axis=1)
    first = lax.slice_in_dim(key_value, 0, frame_rows, axis=1)
    forward = [(s * rep_count + rep_count - 1, (s + 1) * rep_count) for s in range(seq_count - 1)]
    backward = [(s * rep_count, (s - 1) * rep_count + rep_count - 1) for s in range(1, seq_count)]
    low = lax.ppermute(last, ("seq", "rep"), forward)
    high = lax.ppermute(first, ("seq", "rep"), backward)
    return jnp.where(rep_index == 0, low, high)


def per_device(query, key_value, key_blocks):
    frame_rows = BLOCKS_PER_FRAME * MASK_BLOCK_SIZE
    query_count = query.shape[0]
    slab_rows = key_value.shape[1]
    columns = key_value.shape[2]
    head_count = columns // HEAD_WIDTH
    slab_blocks = slab_rows // MASK_BLOCK_SIZE
    slab_frames = slab_rows // frame_rows
    far_count = slab_blocks // FAR_STRIDE
    seq_count = lax.axis_size("seq")
    rep_count = lax.axis_size("rep")
    slab_index = lax.axis_index("seq")
    rep_index = lax.axis_index("rep")
    query_frames = query_count // frame_rows
    query_blocks = query_count // MASK_BLOCK_SIZE
    score_scale = 1.0 / math.sqrt(HEAD_WIDTH)
    assert rep_count >= 2 and query_frames * rep_count == slab_frames
    assert far_count % rep_count == 0
    far_share = far_count // rep_count

    halo = halo_frame(key_value, frame_rows, seq_count, rep_count, rep_index)

    phases = jnp.maximum(key_blocks[0], 0) % FAR_STRIDE
    stride_grid = key_value.reshape(2, far_count, FAR_STRIDE, MASK_BLOCK_SIZE, columns)
    share_grid = lax.dynamic_slice_in_dim(stride_grid, rep_index * far_share, far_share, 1)
    received = []
    pick_list = []
    valid_list = []
    for tier_index in range(LEVELS):
        distance = 2 ** (tier_index + 1)
        if distance >= seq_count:
            continue
        if seq_count <= 2 * distance:
            ahead = [(q, q + distance) for q in range(seq_count - distance)]
            behind = [(q, q - distance) for q in range(distance, seq_count) if q + distance >= seq_count]
            side = (slab_index + distance >= seq_count).astype(jnp.int32)
            slots = [(ahead + behind, side)]
        else:
            ahead = [(q, q + distance) for q in range(seq_count - distance)]
            behind = [(q, q - distance) for q in range(distance, seq_count)]
            slots = [(ahead, jnp.int32(0)), (behind, jnp.int32(1))]
        for pairs, side in slots:
            slot_index = 2 * tier_index + side
            phase = lax.dynamic_index_in_dim(phases, slot_index, 0, keepdims=False)
            wanted = lax.ppermute(phase[None], "seq", pairs)[0]
            chosen = lax.dynamic_index_in_dim(share_grid, wanted, 2, keepdims=False)
            received.append((chosen, [(b, a) for a, b in pairs]))
            partner = slab_index + (1 - 2 * side) * distance
            inside = (partner >= 0) & (partner < seq_count)
            named = lax.dynamic_index_in_dim(key_blocks, slot_index, 1, keepdims=False)
            pick = (named - partner * slab_blocks - phase) // FAR_STRIDE
            pick_list.append(pick)
            valid_list.append((named >= 0) & inside)
    query, payloads = lax.optimization_barrier((query, [chosen for chosen, _ in received]))
    received = [lax.ppermute(chosen, "seq", back) for chosen, (_, back) in zip(payloads, received)]
    slot_count = len(received)
    mine = jnp.stack(received, 1)
    parts = [mine]
    sources = [rep_index]
    for k in range(1, rep_count):
        shift = [(r, (r + k) % rep_count) for r in range(rep_count)]
        parts.append(lax.ppermute(mine, "rep", shift))
        sources.append((rep_index - k) % rep_count)
    far_pair = jnp.stack(parts, 2).reshape(2, slot_count * far_count * MASK_BLOCK_SIZE, columns)
    far_pick = jnp.stack(pick_list, 1)
    far_valid = jnp.stack(valid_list, 1)
    share_ids = jnp.arange(far_share, dtype=jnp.int32)
    candidates = (jnp.stack(sources)[:, None] * far_share + share_ids[None, :]).reshape(far_count)
    far_mask = far_valid[:, :, None] & (far_pick[:, :, None] == candidates[None, None, :])
    far_mask = jnp.repeat(far_mask.reshape(query_blocks, 1, slot_count * far_count), MASK_BLOCK_SIZE, axis=2)

    halo_valid = ((rep_index == 0) & (slab_index > 0)) | (
        (rep_index == rep_count - 1) & (slab_index < seq_count - 1)
    )
    outputs = []
    for head in range(head_count):
        cols = slice(head * HEAD_WIDTH, (head + 1) * HEAD_WIDTH)
        query_head = query[:, cols]
        own_scores = (
            jnp.dot(query_head, key_value[0, :, cols].T, preferred_element_type=jnp.float32)
            * score_scale
        )
        own_top = jnp.max(own_scores, axis=1, keepdims=True)
        own_exp = jnp.exp(own_scores - own_top)
        own_total = jnp.sum(own_exp, axis=1, keepdims=True)
        halo_scores = (
            jnp.dot(query_head, halo[0, :, cols].T, preferred_element_type=jnp.float32)
            * score_scale
        )
        halo_scores = jnp.where(halo_valid, halo_scores, -jnp.inf)
        far_scores = (
            jnp.dot(query_head, far_pair[0, :, cols].T, preferred_element_type=jnp.float32)
            * score_scale
        )
        far_scores = jnp.where(
            far_mask, far_scores.reshape(query_blocks, MASK_BLOCK_SIZE, -1), -jnp.inf
        ).reshape(query_count, -1)
        row_top = jnp.maximum(
            own_top,
            jnp.maximum(
                jnp.max(halo_scores, axis=1, keepdims=True),
                jnp.max(far_scores, axis=1, keepdims=True),
            ),
        )
        own_factor = jnp.exp(own_top - row_top)
        halo_exp = jnp.exp(halo_scores - row_top)
        far_exp = jnp.exp(far_scores - row_top)
        row_total = (
            own_total * own_factor
            + jnp.sum(halo_exp, axis=1, keepdims=True)
            + jnp.sum(far_exp, axis=1, keepdims=True)
        )
        own_prob = (own_exp * (own_factor / row_total)).astype(jnp.bfloat16)
        halo_prob = (halo_exp / row_total).astype(jnp.bfloat16)
        far_prob = (far_exp / row_total).astype(jnp.bfloat16)
        mixed = jnp.dot(own_prob, key_value[1, :, cols], preferred_element_type=jnp.float32)
        mixed = mixed + jnp.dot(halo_prob, halo[1, :, cols], preferred_element_type=jnp.float32)
        mixed = mixed + jnp.dot(far_prob, far_pair[1, :, cols], preferred_element_type=jnp.float32)
        outputs.append(mixed.astype(jnp.bfloat16))
    return jnp.concatenate(outputs, axis=1)


def solution(mesh):
    in_specs = (
        P(("grp", "seq", "rep"), "head"),
        P(None, ("grp", "seq"), "head"),
        P(("grp", "seq", "rep"), None),
    )
    out_specs = P(("grp", "seq", "rep"), "head")
    return jax.shard_map(
        per_device, mesh=mesh, in_specs=in_specs, out_specs=out_specs, check_vma=False
    )
```

```python
import math

import jax
import jax.numpy as jnp
from jax import lax
from jax.sharding import PartitionSpec as P

HEAD_WIDTH = 128
MASK_BLOCK_SIZE = 128
BLOCKS_PER_FRAME = 4
FAR_STRIDE = 4
LEVELS = 4


def from_behind(shard, axis, by):
    count = lax.axis_size(axis)
    pairs = [(i, i + by) for i in range(count) if 0 <= i + by < count]
    return lax.ppermute(shard, axis, pairs)


def halo_frame(key_value, frame_rows, seq_count, rep_count, rep_index):
    slab_rows = key_value.shape[1]
    last = lax.slice_in_dim(key_value, slab_rows - frame_rows, slab_rows, axis=1)
    first = lax.slice_in_dim(key_value, 0, frame_rows, axis=1)
    forward = [(s * rep_count + rep_count - 1, (s + 1) * rep_count) for s in range(seq_count - 1)]
    backward = [(s * rep_count, (s - 1) * rep_count + rep_count - 1) for s in range(1, seq_count)]
    low = lax.ppermute(last, ("seq", "rep"), forward)
    high = lax.ppermute(first, ("seq", "rep"), backward)
    return jnp.where(rep_index == 0, low, high)


def per_device(query, key_value, key_blocks):
    frame_rows = BLOCKS_PER_FRAME * MASK_BLOCK_SIZE
    query_count = query.shape[0]
    slab_rows = key_value.shape[1]
    columns = key_value.shape[2]
    head_count = columns // HEAD_WIDTH
    slab_blocks = slab_rows // MASK_BLOCK_SIZE
    slab_frames = slab_rows // frame_rows
    far_count = slab_blocks // FAR_STRIDE
    seq_count = lax.axis_size("seq")
    rep_count = lax.axis_size("rep")
    slab_index = lax.axis_index("seq")
    rep_index = lax.axis_index("rep")
    query_frames = query_count // frame_rows
    query_blocks = query_count // MASK_BLOCK_SIZE
    score_scale = 1.0 / math.sqrt(HEAD_WIDTH)
    assert rep_count >= 2 and query_frames * rep_count == slab_frames
    assert far_count % rep_count == 0
    far_share = far_count // rep_count

    halo = halo_frame(key_value, frame_rows, seq_count, rep_count, rep_index)

    phases = jnp.maximum(key_blocks[0], 0) % FAR_STRIDE
    stride_grid = key_value.reshape(2, far_count, FAR_STRIDE, MASK_BLOCK_SIZE, columns)
    share_grid = lax.dynamic_slice_in_dim(stride_grid, rep_index * far_share, far_share, 1)
    received = []
    pick_list = []
    valid_list = []
    for tier_index in range(LEVELS):
        distance = 2 ** (tier_index + 1)
        if distance >= seq_count:
            continue
        if seq_count <= 2 * distance:
            ahead = [(q, q + distance) for q in range(seq_count - distance)]
            behind = [(q, q - distance) for q in range(distance, seq_count) if q + distance >= seq_count]
            side = (slab_index + distance >= seq_count).astype(jnp.int32)
            slots = [(ahead + behind, side)]
        else:
            ahead = [(q, q + distance) for q in range(seq_count - distance)]
            behind = [(q, q - distance) for q in range(distance, seq_count)]
            slots = [(ahead, jnp.int32(0)), (behind, jnp.int32(1))]
        for pairs, side in slots:
            slot_index = 2 * tier_index + side
            phase = lax.dynamic_index_in_dim(phases, slot_index, 0, keepdims=False)
            wanted = lax.ppermute(phase[None], "seq", pairs)[0]
            chosen = lax.dynamic_index_in_dim(share_grid, wanted, 2, keepdims=False)
            received.append((chosen, [(b, a) for a, b in pairs]))
            partner = slab_index + (1 - 2 * side) * distance
            inside = (partner >= 0) & (partner < seq_count)
            named = lax.dynamic_index_in_dim(key_blocks, slot_index, 1, keepdims=False)
            pick = (named - partner * slab_blocks - phase) // FAR_STRIDE
            pick_list.append(pick)
            valid_list.append((named >= 0) & inside)
    query, payloads = lax.optimization_barrier((query, [chosen for chosen, _ in received]))
    received = [lax.ppermute(chosen, "seq", back) for chosen, (_, back) in zip(payloads, received)]
    slot_count = len(received)
    halo_valid = ((rep_index == 0) & (slab_index > 0)) | (
        (rep_index == rep_count - 1) & (slab_index < seq_count - 1)
    )

    near = []
    for head in range(head_count):
        cols = slice(head * HEAD_WIDTH, (head + 1) * HEAD_WIDTH)
        query_head = query[:, cols]
        own_scores = (
            jnp.dot(query_head, key_value[0, :, cols].T, preferred_element_type=jnp.float32)
            * score_scale
        )
        halo_scores = (
            jnp.dot(query_head, halo[0, :, cols].T, preferred_element_type=jnp.float32)
            * score_scale
        )
        halo_scores = jnp.where(halo_valid, halo_scores, -jnp.inf)
        near_top = jnp.maximum(
            jnp.max(own_scores, axis=1, keepdims=True), jnp.max(halo_scores, axis=1, keepdims=True)
        )
        own_exp = jnp.exp(own_scores - near_top)
        halo_exp = jnp.exp(halo_scores - near_top)
        near_total = jnp.sum(own_exp, axis=1, keepdims=True) + jnp.sum(
            halo_exp, axis=1, keepdims=True
        )
        near.append((near_top, own_exp, halo_exp, near_total))
    received, near = lax.optimization_barrier((received, near))

    mine = jnp.stack(received, 1)
    parts = [mine]
    sources = [rep_index]
    for k in range(1, rep_count):
        shift = [(r, (r + k) % rep_count) for r in range(rep_count)]
        parts.append(lax.ppermute(mine, "rep", shift))
        sources.append((rep_index - k) % rep_count)
    far_pair = jnp.stack(parts, 2).reshape(2, slot_count * far_count * MASK_BLOCK_SIZE, columns)
    far_pick = jnp.stack(pick_list, 1)
    far_valid = jnp.stack(valid_list, 1)
    share_ids = jnp.arange(far_share, dtype=jnp.int32)
    candidates = (jnp.stack(sources)[:, None] * far_share + share_ids[None, :]).reshape(far_count)
    far_mask = far_valid[:, :, None] & (far_pick[:, :, None] == candidates[None, None, :])
    far_mask = jnp.repeat(far_mask.reshape(query_blocks, 1, slot_count * far_count), MASK_BLOCK_SIZE, axis=2)

    outputs = []
    for head in range(head_count):
        cols = slice(head * HEAD_WIDTH, (head + 1) * HEAD_WIDTH)
        near_top, own_exp, halo_exp, near_total = near[head]
        far_scores = (
            jnp.dot(query[:, cols], far_pair[0, :, cols].T, preferred_element_type=jnp.float32)
            * score_scale
        )
        far_scores = jnp.where(
            far_mask, far_scores.reshape(query_blocks, MASK_BLOCK_SIZE, -1), -jnp.inf
        ).reshape(query_count, -1)
        row_top = jnp.maximum(near_top, jnp.max(far_scores, axis=1, keepdims=True))
        near_factor = jnp.exp(near_top - row_top)
        far_exp = jnp.exp(far_scores - row_top)
        row_total = near_total * near_factor + jnp.sum(far_exp, axis=1, keepdims=True)
        near_scale = near_factor / row_total
        own_prob = (own_exp * near_scale).astype(jnp.bfloat16)
        halo_prob = (halo_exp * near_scale).astype(jnp.bfloat16)
        far_prob = (far_exp / row_total).astype(jnp.bfloat16)
        mixed = jnp.dot(own_prob, key_value[1, :, cols], preferred_element_type=jnp.float32)
        mixed = mixed + jnp.dot(halo_prob, halo[1, :, cols], preferred_element_type=jnp.float32)
        mixed = mixed + jnp.dot(far_prob, far_pair[1, :, cols], preferred_element_type=jnp.float32)
        outputs.append(mixed.astype(jnp.bfloat16))
    return jnp.concatenate(outputs, axis=1)


def solution(mesh):
    in_specs = (
        P(("grp", "seq", "rep"), "head"),
        P(None, ("grp", "seq"), "head"),
        P(("grp", "seq", "rep"), None),
    )
    out_specs = P(("grp", "seq", "rep"), "head")
    return jax.shard_map(
        per_device, mesh=mesh, in_specs=in_specs, out_specs=out_specs, check_vma=False
    )
```

```python
import math

import jax
import jax.numpy as jnp
from jax import lax
from jax.sharding import PartitionSpec as P

HEAD_WIDTH = 128
MASK_BLOCK_SIZE = 128
BLOCKS_PER_FRAME = 4
FAR_STRIDE = 4
LEVELS = 4


def from_behind(shard, axis, by):
    count = lax.axis_size(axis)
    pairs = [(i, i + by) for i in range(count) if 0 <= i + by < count]
    return lax.ppermute(shard, axis, pairs)


def halo_frame(key_value, frame_rows, seq_count, rep_count, rep_index):
    slab_rows = key_value.shape[1]
    last = lax.slice_in_dim(key_value, slab_rows - frame_rows, slab_rows, axis=1)
    first = lax.slice_in_dim(key_value, 0, frame_rows, axis=1)
    forward = [(s * rep_count + rep_count - 1, (s + 1) * rep_count) for s in range(seq_count - 1)]
    backward = [(s * rep_count, (s - 1) * rep_count + rep_count - 1) for s in range(1, seq_count)]
    low = lax.ppermute(last, ("seq", "rep"), forward)
    high = lax.ppermute(first, ("seq", "rep"), backward)
    return jnp.where(rep_index == 0, low, high)


def send_far(chosen, pairs):
    if any(abs(b - a) != 2 for a, b in pairs):
        return lax.ppermute(chosen, "seq", pairs)
    total = None
    for sign in (1, -1):
        moving = [(a, b) for a, b in pairs if (b - a) * sign > 0]
        if not moving:
            continue
        hop = lax.ppermute(chosen, "seq", [(a, a + sign) for a, _ in moving])
        hop = lax.ppermute(hop, "seq", [(a + sign, b) for a, b in moving])
        total = hop if total is None else total + hop
    return total


def per_device(query, key_value, key_blocks):
    frame_rows = BLOCKS_PER_FRAME * MASK_BLOCK_SIZE
    query_count = query.shape[0]
    slab_rows = key_value.shape[1]
    columns = key_value.shape[2]
    head_count = columns // HEAD_WIDTH
    slab_blocks = slab_rows // MASK_BLOCK_SIZE
    slab_frames = slab_rows // frame_rows
    far_count = slab_blocks // FAR_STRIDE
    seq_count = lax.axis_size("seq")
    rep_count = lax.axis_size("rep")
    slab_index = lax.axis_index("seq")
    rep_index = lax.axis_index("rep")
    query_frames = query_count // frame_rows
    query_blocks = query_count // MASK_BLOCK_SIZE
    score_scale = 1.0 / math.sqrt(HEAD_WIDTH)
    assert rep_count >= 2 and query_frames * rep_count == slab_frames
    assert far_count % rep_count == 0
    far_share = far_count // rep_count

    halo = halo_frame(key_value, frame_rows, seq_count, rep_count, rep_index)

    phases = jnp.maximum(key_blocks[0], 0) % FAR_STRIDE
    stride_grid = key_value.reshape(2, far_count, FAR_STRIDE, MASK_BLOCK_SIZE, columns)
    share_grid = lax.dynamic_slice_in_dim(stride_grid, rep_index * far_share, far_share, 1)
    received = []
    pick_list = []
    valid_list = []
    for tier_index in range(LEVELS):
        distance = 2 ** (tier_index + 1)
        if distance >= seq_count:
            continue
        if seq_count <= 2 * distance:
            ahead = [(q, q + distance) for q in range(seq_count - distance)]
            behind = [(q, q - distance) for q in range(distance, seq_count) if q + distance >= seq_count]
            side = (slab_index + distance >= seq_count).astype(jnp.int32)
            slots = [(ahead + behind, side)]
        else:
            ahead = [(q, q + distance) for q in range(seq_count - distance)]
            behind = [(q, q - distance) for q in range(distance, seq_count)]
            slots = [(ahead, jnp.int32(0)), (behind, jnp.int32(1))]
        for pairs, side in slots:
            slot_index = 2 * tier_index + side
            phase = lax.dynamic_index_in_dim(phases, slot_index, 0, keepdims=False)
            wanted = lax.ppermute(phase[None], "seq", pairs)[0]
            chosen = lax.dynamic_index_in_dim(share_grid, wanted, 2, keepdims=False)
            received.append((chosen, [(b, a) for a, b in pairs]))
            partner = slab_index + (1 - 2 * side) * distance
            inside = (partner >= 0) & (partner < seq_count)
            named = lax.dynamic_index_in_dim(key_blocks, slot_index, 1, keepdims=False)
            pick = (named - partner * slab_blocks - phase) // FAR_STRIDE
            pick_list.append(pick)
            valid_list.append((named >= 0) & inside)
    query, payloads = lax.optimization_barrier((query, [chosen for chosen, _ in received]))
    received = [send_far(chosen, back) for chosen, (_, back) in zip(payloads, received)]
    slot_count = len(received)
    halo_valid = ((rep_index == 0) & (slab_index > 0)) | (
        (rep_index == rep_count - 1) & (slab_index < seq_count - 1)
    )

    near = []
    for head in range(head_count):
        cols = slice(head * HEAD_WIDTH, (head + 1) * HEAD_WIDTH)
        query_head = query[:, cols]
        own_scores = (
            jnp.dot(query_head, key_value[0, :, cols].T, preferred_element_type=jnp.float32)
            * score_scale
        )
        halo_scores = (
            jnp.dot(query_head, halo[0, :, cols].T, preferred_element_type=jnp.float32)
            * score_scale
        )
        halo_scores = jnp.where(halo_valid, halo_scores, -jnp.inf)
        near_top = jnp.maximum(
            jnp.max(own_scores, axis=1, keepdims=True), jnp.max(halo_scores, axis=1, keepdims=True)
        )
        own_exp = jnp.exp(own_scores - near_top)
        halo_exp = jnp.exp(halo_scores - near_top)
        near_total = jnp.sum(own_exp, axis=1, keepdims=True) + jnp.sum(
            halo_exp, axis=1, keepdims=True
        )
        near.append((near_top, own_exp, halo_exp, near_total))
    received, near = lax.optimization_barrier((received, near))

    mine = jnp.stack(received, 1)
    parts = [mine]
    sources = [rep_index]
    for k in range(1, rep_count):
        shift = [(r, (r + k) % rep_count) for r in range(rep_count)]
        parts.append(lax.ppermute(mine, "rep", shift))
        sources.append((rep_index - k) % rep_count)
    far_pair = jnp.stack(parts, 2).reshape(2, slot_count * far_count * MASK_BLOCK_SIZE, columns)
    far_pick = jnp.stack(pick_list, 1)
    far_valid = jnp.stack(valid_list, 1)
    share_ids = jnp.arange(far_share, dtype=jnp.int32)
    candidates = (jnp.stack(sources)[:, None] * far_share + share_ids[None, :]).reshape(far_count)
    far_mask = far_valid[:, :, None] & (far_pick[:, :, None] == candidates[None, None, :])
    far_mask = jnp.repeat(far_mask.reshape(query_blocks, 1, slot_count * far_count), MASK_BLOCK_SIZE, axis=2)

    outputs = []
    for head in range(head_count):
        cols = slice(head * HEAD_WIDTH, (head + 1) * HEAD_WIDTH)
        near_top, own_exp, halo_exp, near_total = near[head]
        far_scores = (
            jnp.dot(query[:, cols], far_pair[0, :, cols].T, preferred_element_type=jnp.float32)
            * score_scale
        )
        far_scores = jnp.where(
            far_mask, far_scores.reshape(query_blocks, MASK_BLOCK_SIZE, -1), -jnp.inf
        ).reshape(query_count, -1)
        row_top = jnp.maximum(near_top, jnp.max(far_scores, axis=1, keepdims=True))
        near_factor = jnp.exp(near_top - row_top)
        far_exp = jnp.exp(far_scores - row_top)
        row_total = near_total * near_factor + jnp.sum(far_exp, axis=1, keepdims=True)
        near_scale = near_factor / row_total
        own_prob = (own_exp * near_scale).astype(jnp.bfloat16)
        halo_prob = (halo_exp * near_scale).astype(jnp.bfloat16)
        far_prob = (far_exp / row_total).astype(jnp.bfloat16)
        mixed = jnp.dot(own_prob, key_value[1, :, cols], preferred_element_type=jnp.float32)
        mixed = mixed + jnp.dot(halo_prob, halo[1, :, cols], preferred_element_type=jnp.float32)
        mixed = mixed + jnp.dot(far_prob, far_pair[1, :, cols], preferred_element_type=jnp.float32)
        outputs.append(mixed.astype(jnp.bfloat16))
    return jnp.concatenate(outputs, axis=1)


def solution(mesh):
    in_specs = (
        P(("grp", "seq", "rep"), "head"),
        P(None, ("grp", "seq"), "head"),
        P(("grp", "seq", "rep"), None),
    )
    out_specs = P(("grp", "seq", "rep"), "head")
    return jax.shard_map(
        per_device, mesh=mesh, in_specs=in_specs, out_specs=out_specs, check_vma=False
    )
```

```python
import math

import jax
import jax.numpy as jnp
from jax import lax
from jax.sharding import PartitionSpec as P

HEAD_WIDTH = 128
MASK_BLOCK_SIZE = 128
BLOCKS_PER_FRAME = 4
FAR_STRIDE = 4
LEVELS = 4


def from_behind(shard, axis, by):
    count = lax.axis_size(axis)
    pairs = [(i, i + by) for i in range(count) if 0 <= i + by < count]
    return lax.ppermute(shard, axis, pairs)


def halo_frame(key_value, key_blocks, frame_rows, seq_count, rep_count, rep_index):
    slab_rows = key_value.shape[1]
    last = lax.slice_in_dim(key_value, slab_rows - frame_rows, slab_rows, axis=1)
    first = lax.slice_in_dim(key_value, 0, frame_rows, axis=1)
    key_blocks, last, first = lax.optimization_barrier((key_blocks, last, first))
    forward = [(s * rep_count + rep_count - 1, (s + 1) * rep_count) for s in range(seq_count - 1)]
    backward = [(s * rep_count, (s - 1) * rep_count + rep_count - 1) for s in range(1, seq_count)]
    low = lax.ppermute(last, ("seq", "rep"), forward)
    high = lax.ppermute(first, ("seq", "rep"), backward)
    return jnp.where(rep_index == 0, low, high), key_blocks


def per_device(query, key_value, key_blocks):
    frame_rows = BLOCKS_PER_FRAME * MASK_BLOCK_SIZE
    query_count = query.shape[0]
    slab_rows = key_value.shape[1]
    columns = key_value.shape[2]
    head_count = columns // HEAD_WIDTH
    slab_blocks = slab_rows // MASK_BLOCK_SIZE
    slab_frames = slab_rows // frame_rows
    far_count = slab_blocks // FAR_STRIDE
    seq_count = lax.axis_size("seq")
    rep_count = lax.axis_size("rep")
    slab_index = lax.axis_index("seq")
    rep_index = lax.axis_index("rep")
    query_frames = query_count // frame_rows
    query_blocks = query_count // MASK_BLOCK_SIZE
    score_scale = 1.0 / math.sqrt(HEAD_WIDTH)
    assert rep_count >= 2 and query_frames * rep_count == slab_frames
    assert far_count % rep_count == 0
    far_share = far_count // rep_count

    halo, key_blocks = halo_frame(key_value, key_blocks, frame_rows, seq_count, rep_count, rep_index)

    phases = jnp.maximum(key_blocks[0], 0) % FAR_STRIDE
    stride_grid = key_value.reshape(2, far_count, FAR_STRIDE, MASK_BLOCK_SIZE, columns)
    share_grid = lax.dynamic_slice_in_dim(stride_grid, rep_index * far_share, far_share, 1)
    received = []
    pick_list = []
    valid_list = []
    for tier_index in range(LEVELS):
        distance = 2 ** (tier_index + 1)
        if distance >= seq_count:
            continue
        if seq_count <= 2 * distance:
            ahead = [(q, q + distance) for q in range(seq_count - distance)]
            behind = [(q, q - distance) for q in range(distance, seq_count) if q + distance >= seq_count]
            side = (slab_index + distance >= seq_count).astype(jnp.int32)
            slots = [(ahead + behind, side)]
        else:
            ahead = [(q, q + distance) for q in range(seq_count - distance)]
            behind = [(q, q - distance) for q in range(distance, seq_count)]
            slots = [(ahead, jnp.int32(0)), (behind, jnp.int32(1))]
        for pairs, side in slots:
            slot_index = 2 * tier_index + side
            phase = lax.dynamic_index_in_dim(phases, slot_index, 0, keepdims=False)
            wanted = lax.ppermute(phase[None], "seq", pairs)[0]
            chosen = lax.dynamic_index_in_dim(share_grid, wanted, 2, keepdims=False)
            received.append((chosen, [(b, a) for a, b in pairs]))
            partner = slab_index + (1 - 2 * side) * distance
            inside = (partner >= 0) & (partner < seq_count)
            named = lax.dynamic_index_in_dim(key_blocks, slot_index, 1, keepdims=False)
            pick = (named - partner * slab_blocks - phase) // FAR_STRIDE
            pick_list.append(pick)
            valid_list.append((named >= 0) & inside)
    query, payloads = lax.optimization_barrier((query, [chosen for chosen, _ in received]))
    received = [lax.ppermute(chosen, "seq", back) for chosen, (_, back) in zip(payloads, received)]
    slot_count = len(received)
    halo_valid = ((rep_index == 0) & (slab_index > 0)) | (
        (rep_index == rep_count - 1) & (slab_index < seq_count - 1)
    )

    near = []
    for head in range(head_count):
        cols = slice(head * HEAD_WIDTH, (head + 1) * HEAD_WIDTH)
        query_head = query[:, cols]
        own_scores = (
            jnp.dot(query_head, key_value[0, :, cols].T, preferred_element_type=jnp.float32)
            * score_scale
        )
        halo_scores = (
            jnp.dot(query_head, halo[0, :, cols].T, preferred_element_type=jnp.float32)
            * score_scale
        )
        halo_scores = jnp.where(halo_valid, halo_scores, -jnp.inf)
        near_top = jnp.maximum(
            jnp.max(own_scores, axis=1, keepdims=True), jnp.max(halo_scores, axis=1, keepdims=True)
        )
        own_exp = jnp.exp(own_scores - near_top)
        halo_exp = jnp.exp(halo_scores - near_top)
        near_total = jnp.sum(own_exp, axis=1, keepdims=True) + jnp.sum(
            halo_exp, axis=1, keepdims=True
        )
        near.append((near_top, own_exp, halo_exp, near_total))
    received, near = lax.optimization_barrier((received, near))

    mine = jnp.stack(received, 1)
    parts = [mine]
    sources = [rep_index]
    for k in range(1, rep_count):
        shift = [(r, (r + k) % rep_count) for r in range(rep_count)]
        parts.append(lax.ppermute(mine, "rep", shift))
        sources.append((rep_index - k) % rep_count)
    far_pair = jnp.stack(parts, 2).reshape(2, slot_count * far_count * MASK_BLOCK_SIZE, columns)
    far_pick = jnp.stack(pick_list, 1)
    far_valid = jnp.stack(valid_list, 1)
    share_ids = jnp.arange(far_share, dtype=jnp.int32)
    candidates = (jnp.stack(sources)[:, None] * far_share + share_ids[None, :]).reshape(far_count)
    far_mask = far_valid[:, :, None] & (far_pick[:, :, None] == candidates[None, None, :])
    far_mask = jnp.repeat(far_mask.reshape(query_blocks, 1, slot_count * far_count), MASK_BLOCK_SIZE, axis=2)

    outputs = []
    for head in range(head_count):
        cols = slice(head * HEAD_WIDTH, (head + 1) * HEAD_WIDTH)
        near_top, own_exp, halo_exp, near_total = near[head]
        far_scores = (
            jnp.dot(query[:, cols], far_pair[0, :, cols].T, preferred_element_type=jnp.float32)
            * score_scale
        )
        far_scores = jnp.where(
            far_mask, far_scores.reshape(query_blocks, MASK_BLOCK_SIZE, -1), -jnp.inf
        ).reshape(query_count, -1)
        row_top = jnp.maximum(near_top, jnp.max(far_scores, axis=1, keepdims=True))
        near_factor = jnp.exp(near_top - row_top)
        far_exp = jnp.exp(far_scores - row_top)
        row_total = near_total * near_factor + jnp.sum(far_exp, axis=1, keepdims=True)
        near_scale = near_factor / row_total
        own_prob = (own_exp * near_scale).astype(jnp.bfloat16)
        halo_prob = (halo_exp * near_scale).astype(jnp.bfloat16)
        far_prob = (far_exp / row_total).astype(jnp.bfloat16)
        mixed = jnp.dot(own_prob, key_value[1, :, cols], preferred_element_type=jnp.float32)
        mixed = mixed + jnp.dot(halo_prob, halo[1, :, cols], preferred_element_type=jnp.float32)
        mixed = mixed + jnp.dot(far_prob, far_pair[1, :, cols], preferred_element_type=jnp.float32)
        outputs.append(mixed.astype(jnp.bfloat16))
    return jnp.concatenate(outputs, axis=1)


def solution(mesh):
    in_specs = (
        P(("grp", "seq", "rep"), "head"),
        P(None, ("grp", "seq"), "head"),
        P(("grp", "seq", "rep"), None),
    )
    out_specs = P(("grp", "seq", "rep"), "head")
    return jax.shard_map(
        per_device, mesh=mesh, in_specs=in_specs, out_specs=out_specs, check_vma=False
    )
```

```python
import math

import jax
import jax.numpy as jnp
from jax import lax
from jax.sharding import PartitionSpec as P

HEAD_WIDTH = 128
MASK_BLOCK_SIZE = 128
BLOCKS_PER_FRAME = 4
FAR_STRIDE = 4
LEVELS = 4


def from_behind(shard, axis, by):
    count = lax.axis_size(axis)
    pairs = [(i, i + by) for i in range(count) if 0 <= i + by < count]
    return lax.ppermute(shard, axis, pairs)


def halo_frame(key_value, key_blocks, frame_rows, seq_count, rep_count, rep_index):
    slab_rows = key_value.shape[1]
    start = jnp.where(rep_index == rep_count - 1, slab_rows - frame_rows, 0)
    payload = lax.dynamic_slice_in_dim(key_value, start, frame_rows, 1)
    key_blocks, payload = lax.optimization_barrier((key_blocks, payload))
    pairs = [(s * rep_count + rep_count - 1, (s + 1) * rep_count) for s in range(seq_count - 1)]
    pairs += [(s * rep_count, (s - 1) * rep_count + rep_count - 1) for s in range(1, seq_count)]
    return lax.ppermute(payload, ("seq", "rep"), pairs), key_blocks


def per_device(query, key_value, key_blocks):
    frame_rows = BLOCKS_PER_FRAME * MASK_BLOCK_SIZE
    query_count = query.shape[0]
    slab_rows = key_value.shape[1]
    columns = key_value.shape[2]
    head_count = columns // HEAD_WIDTH
    slab_blocks = slab_rows // MASK_BLOCK_SIZE
    slab_frames = slab_rows // frame_rows
    far_count = slab_blocks // FAR_STRIDE
    seq_count = lax.axis_size("seq")
    rep_count = lax.axis_size("rep")
    slab_index = lax.axis_index("seq")
    rep_index = lax.axis_index("rep")
    query_frames = query_count // frame_rows
    query_blocks = query_count // MASK_BLOCK_SIZE
    score_scale = 1.0 / math.sqrt(HEAD_WIDTH)
    assert rep_count >= 2 and query_frames * rep_count == slab_frames
    assert far_count % rep_count == 0
    far_share = far_count // rep_count

    halo, key_blocks = halo_frame(key_value, key_blocks, frame_rows, seq_count, rep_count, rep_index)

    phases = jnp.maximum(key_blocks[0], 0) % FAR_STRIDE
    stride_grid = key_value.reshape(2, far_count, FAR_STRIDE, MASK_BLOCK_SIZE, columns)
    share_grid = lax.dynamic_slice_in_dim(stride_grid, rep_index * far_share, far_share, 1)
    received = []
    pick_list = []
    valid_list = []
    for tier_index in range(LEVELS):
        distance = 2 ** (tier_index + 1)
        if distance >= seq_count:
            continue
        if seq_count <= 2 * distance:
            ahead = [(q, q + distance) for q in range(seq_count - distance)]
            behind = [(q, q - distance) for q in range(distance, seq_count) if q + distance >= seq_count]
            side = (slab_index + distance >= seq_count).astype(jnp.int32)
            slots = [(ahead + behind, side)]
        else:
            ahead = [(q, q + distance) for q in range(seq_count - distance)]
            behind = [(q, q - distance) for q in range(distance, seq_count)]
            slots = [(ahead, jnp.int32(0)), (behind, jnp.int32(1))]
        for pairs, side in slots:
            slot_index = 2 * tier_index + side
            phase = lax.dynamic_index_in_dim(phases, slot_index, 0, keepdims=False)
            wanted = lax.ppermute(phase[None], "seq", pairs)[0]
            chosen = lax.dynamic_index_in_dim(share_grid, wanted, 2, keepdims=False)
            received.append((chosen, [(b, a) for a, b in pairs]))
            partner = slab_index + (1 - 2 * side) * distance
            inside = (partner >= 0) & (partner < seq_count)
            named = lax.dynamic_index_in_dim(key_blocks, slot_index, 1, keepdims=False)
            pick = (named - partner * slab_blocks - phase) // FAR_STRIDE
            pick_list.append(pick)
            valid_list.append((named >= 0) & inside)
    query, payloads = lax.optimization_barrier((query, [chosen for chosen, _ in received]))
    received = [lax.ppermute(chosen, "seq", back) for chosen, (_, back) in zip(payloads, received)]
    slot_count = len(received)
    halo_valid = ((rep_index == 0) & (slab_index > 0)) | (
        (rep_index == rep_count - 1) & (slab_index < seq_count - 1)
    )

    near = []
    for head in range(head_count):
        cols = slice(head * HEAD_WIDTH, (head + 1) * HEAD_WIDTH)
        query_head = query[:, cols]
        own_scores = (
            jnp.dot(query_head, key_value[0, :, cols].T, preferred_element_type=jnp.float32)
            * score_scale
        )
        halo_scores = (
            jnp.dot(query_head, halo[0, :, cols].T, preferred_element_type=jnp.float32)
            * score_scale
        )
        halo_scores = jnp.where(halo_valid, halo_scores, -jnp.inf)
        near_top = jnp.maximum(
            jnp.max(own_scores, axis=1, keepdims=True), jnp.max(halo_scores, axis=1, keepdims=True)
        )
        own_exp = jnp.exp(own_scores - near_top)
        halo_exp = jnp.exp(halo_scores - near_top)
        near_total = jnp.sum(own_exp, axis=1, keepdims=True) + jnp.sum(
            halo_exp, axis=1, keepdims=True
        )
        near.append((near_top, own_exp, halo_exp, near_total))
    received, near = lax.optimization_barrier((received, near))

    mine = jnp.stack(received, 1)
    parts = [mine]
    sources = [rep_index]
    for k in range(1, rep_count):
        shift = [(r, (r + k) % rep_count) for r in range(rep_count)]
        parts.append(lax.ppermute(mine, "rep", shift))
        sources.append((rep_index - k) % rep_count)
    far_pair = jnp.stack(parts, 2).reshape(2, slot_count * far_count * MASK_BLOCK_SIZE, columns)
    far_pick = jnp.stack(pick_list, 1)
    far_valid = jnp.stack(valid_list, 1)
    share_ids = jnp.arange(far_share, dtype=jnp.int32)
    candidates = (jnp.stack(sources)[:, None] * far_share + share_ids[None, :]).reshape(far_count)
    far_mask = far_valid[:, :, None] & (far_pick[:, :, None] == candidates[None, None, :])
    far_mask = jnp.repeat(far_mask.reshape(query_blocks, 1, slot_count * far_count), MASK_BLOCK_SIZE, axis=2)

    outputs = []
    for head in range(head_count):
        cols = slice(head * HEAD_WIDTH, (head + 1) * HEAD_WIDTH)
        near_top, own_exp, halo_exp, near_total = near[head]
        far_scores = (
            jnp.dot(query[:, cols], far_pair[0, :, cols].T, preferred_element_type=jnp.float32)
            * score_scale
        )
        far_scores = jnp.where(
            far_mask, far_scores.reshape(query_blocks, MASK_BLOCK_SIZE, -1), -jnp.inf
        ).reshape(query_count, -1)
        row_top = jnp.maximum(near_top, jnp.max(far_scores, axis=1, keepdims=True))
        near_factor = jnp.exp(near_top - row_top)
        far_exp = jnp.exp(far_scores - row_top)
        row_total = near_total * near_factor + jnp.sum(far_exp, axis=1, keepdims=True)
        near_scale = near_factor / row_total
        own_prob = (own_exp * near_scale).astype(jnp.bfloat16)
        halo_prob = (halo_exp * near_scale).astype(jnp.bfloat16)
        far_prob = (far_exp / row_total).astype(jnp.bfloat16)
        mixed = jnp.dot(own_prob, key_value[1, :, cols], preferred_element_type=jnp.float32)
        mixed = mixed + jnp.dot(halo_prob, halo[1, :, cols], preferred_element_type=jnp.float32)
        mixed = mixed + jnp.dot(far_prob, far_pair[1, :, cols], preferred_element_type=jnp.float32)
        outputs.append(mixed.astype(jnp.bfloat16))
    return jnp.concatenate(outputs, axis=1)


def solution(mesh):
    in_specs = (
        P(("grp", "seq", "rep"), "head"),
        P(None, ("grp", "seq"), "head"),
        P(("grp", "seq", "rep"), None),
    )
    out_specs = P(("grp", "seq", "rep"), "head")
    return jax.shard_map(
        per_device, mesh=mesh, in_specs=in_specs, out_specs=out_specs, check_vma=False
    )
```

```python
import math

import jax
import jax.numpy as jnp
from jax import lax
from jax.sharding import PartitionSpec as P

HEAD_WIDTH = 128
MASK_BLOCK_SIZE = 128
BLOCKS_PER_FRAME = 4
FAR_STRIDE = 4
LEVELS = 4


def from_behind(shard, axis, by):
    count = lax.axis_size(axis)
    pairs = [(i, i + by) for i in range(count) if 0 <= i + by < count]
    return lax.ppermute(shard, axis, pairs)


def halo_frame(key_value, key_blocks, frame_rows, seq_count, rep_count, rep_index):
    slab_rows = key_value.shape[1]
    start = jnp.where(rep_index == rep_count - 1, slab_rows - frame_rows, 0)
    payload = lax.dynamic_slice_in_dim(key_value, start, frame_rows, 1)
    key_blocks, payload = lax.optimization_barrier((key_blocks, payload))
    pairs = [(s * rep_count + rep_count - 1, (s + 1) * rep_count) for s in range(seq_count - 1)]
    pairs += [(s * rep_count, (s - 1) * rep_count + rep_count - 1) for s in range(1, seq_count)]
    return lax.ppermute(payload, ("seq", "rep"), pairs), key_blocks


def per_device(query, key_value, key_blocks):
    frame_rows = BLOCKS_PER_FRAME * MASK_BLOCK_SIZE
    query_count = query.shape[0]
    slab_rows = key_value.shape[1]
    columns = key_value.shape[2]
    head_count = columns // HEAD_WIDTH
    slab_blocks = slab_rows // MASK_BLOCK_SIZE
    slab_frames = slab_rows // frame_rows
    far_count = slab_blocks // FAR_STRIDE
    seq_count = lax.axis_size("seq")
    rep_count = lax.axis_size("rep")
    slab_index = lax.axis_index("seq")
    rep_index = lax.axis_index("rep")
    query_frames = query_count // frame_rows
    query_blocks = query_count // MASK_BLOCK_SIZE
    score_scale = 1.0 / math.sqrt(HEAD_WIDTH)
    assert rep_count >= 2 and query_frames * rep_count == slab_frames
    assert far_count % rep_count == 0
    far_share = far_count // rep_count

    halo, key_blocks = halo_frame(key_value, key_blocks, frame_rows, seq_count, rep_count, rep_index)
    halo_valid = ((rep_index == 0) & (slab_index > 0)) | (
        (rep_index == rep_count - 1) & (slab_index < seq_count - 1)
    )
    halo = jnp.where(halo_valid, halo, jnp.zeros_like(halo))

    phases = jnp.maximum(key_blocks[0], 0) % FAR_STRIDE
    stride_grid = key_value.reshape(2, far_count, FAR_STRIDE, MASK_BLOCK_SIZE, columns)
    share_grid = lax.dynamic_slice_in_dim(stride_grid, rep_index * far_share, far_share, 1)
    received = []
    pick_list = []
    valid_list = []
    for tier_index in range(LEVELS):
        distance = 2 ** (tier_index + 1)
        if distance >= seq_count:
            continue
        if seq_count <= 2 * distance:
            ahead = [(q, q + distance) for q in range(seq_count - distance)]
            behind = [(q, q - distance) for q in range(distance, seq_count) if q + distance >= seq_count]
            side = (slab_index + distance >= seq_count).astype(jnp.int32)
            slots = [(ahead + behind, side)]
        else:
            ahead = [(q, q + distance) for q in range(seq_count - distance)]
            behind = [(q, q - distance) for q in range(distance, seq_count)]
            slots = [(ahead, jnp.int32(0)), (behind, jnp.int32(1))]
        for pairs, side in slots:
            slot_index = 2 * tier_index + side
            phase = lax.dynamic_index_in_dim(phases, slot_index, 0, keepdims=False)
            wanted = lax.ppermute(phase[None], "seq", pairs)[0]
            chosen = lax.dynamic_index_in_dim(share_grid, wanted, 2, keepdims=False)
            received.append((chosen, [(b, a) for a, b in pairs]))
            partner = slab_index + (1 - 2 * side) * distance
            inside = (partner >= 0) & (partner < seq_count)
            named = lax.dynamic_index_in_dim(key_blocks, slot_index, 1, keepdims=False)
            pick = (named - partner * slab_blocks - phase) // FAR_STRIDE
            pick_list.append(pick)
            valid_list.append((named >= 0) & inside)
    query, payloads = lax.optimization_barrier((query, [chosen for chosen, _ in received]))
    received = [lax.ppermute(chosen, "seq", back) for chosen, (_, back) in zip(payloads, received)]
    slot_count = len(received)

    near = []
    for head in range(head_count):
        cols = slice(head * HEAD_WIDTH, (head + 1) * HEAD_WIDTH)
        query_head = query[:, cols]
        own_scores = (
            jnp.dot(query_head, key_value[0, :, cols].T, preferred_element_type=jnp.float32)
            * score_scale
        )
        halo_scores = (
            jnp.dot(query_head, halo[0, :, cols].T, preferred_element_type=jnp.float32)
            * score_scale
        )
        halo_scores = jnp.where(halo_valid, halo_scores, -jnp.inf)
        near_top = jnp.maximum(
            jnp.max(own_scores, axis=1, keepdims=True), jnp.max(halo_scores, axis=1, keepdims=True)
        )
        own_exp = jnp.exp(own_scores - near_top)
        halo_exp = jnp.exp(halo_scores - near_top)
        near_total = jnp.sum(own_exp, axis=1, keepdims=True) + jnp.sum(
            halo_exp, axis=1, keepdims=True
        )
        near.append((near_top, own_exp, halo_exp, near_total))
    received, near = lax.optimization_barrier((received, near))

    mine = jnp.stack(received, 1)
    parts = [mine]
    sources = [rep_index]
    for k in range(1, rep_count):
        shift = [(r, (r + k) % rep_count) for r in range(rep_count)]
        parts.append(lax.ppermute(mine, "rep", shift))
        sources.append((rep_index - k) % rep_count)
    far_pair = jnp.stack(parts, 2).reshape(2, slot_count * far_count * MASK_BLOCK_SIZE, columns)
    far_pick = jnp.stack(pick_list, 1)
    far_valid = jnp.stack(valid_list, 1)
    share_ids = jnp.arange(far_share, dtype=jnp.int32)
    candidates = (jnp.stack(sources)[:, None] * far_share + share_ids[None, :]).reshape(far_count)
    far_mask = far_valid[:, :, None] & (far_pick[:, :, None] == candidates[None, None, :])
    far_mask = jnp.repeat(far_mask.reshape(query_blocks, 1, slot_count * far_count), MASK_BLOCK_SIZE, axis=2)

    outputs = []
    for head in range(head_count):
        cols = slice(head * HEAD_WIDTH, (head + 1) * HEAD_WIDTH)
        near_top, own_exp, halo_exp, near_total = near[head]
        far_scores = (
            jnp.dot(query[:, cols], far_pair[0, :, cols].T, preferred_element_type=jnp.float32)
            * score_scale
        )
        far_scores = jnp.where(
            far_mask, far_scores.reshape(query_blocks, MASK_BLOCK_SIZE, -1), -jnp.inf
        ).reshape(query_count, -1)
        row_top = jnp.maximum(near_top, jnp.max(far_scores, axis=1, keepdims=True))
        near_factor = jnp.exp(near_top - row_top)
        far_exp = jnp.exp(far_scores - row_top)
        row_total = near_total * near_factor + jnp.sum(far_exp, axis=1, keepdims=True)
        near_scale = near_factor / row_total
        own_prob = (own_exp * near_scale).astype(jnp.bfloat16)
        halo_prob = (halo_exp * near_scale).astype(jnp.bfloat16)
        far_prob = (far_exp / row_total).astype(jnp.bfloat16)
        mixed = jnp.dot(own_prob, key_value[1, :, cols], preferred_element_type=jnp.float32)
        mixed = mixed + jnp.dot(halo_prob, halo[1, :, cols], preferred_element_type=jnp.float32)
        mixed = mixed + jnp.dot(far_prob, far_pair[1, :, cols], preferred_element_type=jnp.float32)
        outputs.append(mixed.astype(jnp.bfloat16))
    return jnp.concatenate(outputs, axis=1)


def solution(mesh):
    in_specs = (
        P(("grp", "seq", "rep"), "head"),
        P(None, ("grp", "seq"), "head"),
        P(("grp", "seq", "rep"), None),
    )
    out_specs = P(("grp", "seq", "rep"), "head")
    return jax.shard_map(
        per_device, mesh=mesh, in_specs=in_specs, out_specs=out_specs, check_vma=False
    )
```

```python
import math

import jax
import jax.numpy as jnp
from jax import lax
from jax.sharding import PartitionSpec as P

HEAD_WIDTH = 128
MASK_BLOCK_SIZE = 128
BLOCKS_PER_FRAME = 4
FAR_STRIDE = 4
LEVELS = 4


def from_behind(shard, axis, by):
    count = lax.axis_size(axis)
    pairs = [(i, i + by) for i in range(count) if 0 <= i + by < count]
    return lax.ppermute(shard, axis, pairs)


def halo_frame(key_value, key_blocks, frame_rows, seq_count, rep_count, rep_index):
    slab_rows = key_value.shape[1]
    start = jnp.where(rep_index == rep_count - 1, slab_rows - frame_rows, 0)
    payload = lax.dynamic_slice_in_dim(key_value, start, frame_rows, 1)
    key_blocks, payload = lax.optimization_barrier((key_blocks, payload))
    pairs = [(s * rep_count + rep_count - 1, (s + 1) * rep_count) for s in range(seq_count - 1)]
    pairs += [(s * rep_count, (s - 1) * rep_count + rep_count - 1) for s in range(1, seq_count)]
    return lax.ppermute(payload, ("seq", "rep"), pairs), key_blocks


def per_device(query, key_value, key_blocks):
    frame_rows = BLOCKS_PER_FRAME * MASK_BLOCK_SIZE
    query_count = query.shape[0]
    slab_rows = key_value.shape[1]
    columns = key_value.shape[2]
    head_count = columns // HEAD_WIDTH
    slab_blocks = slab_rows // MASK_BLOCK_SIZE
    slab_frames = slab_rows // frame_rows
    far_count = slab_blocks // FAR_STRIDE
    seq_count = lax.axis_size("seq")
    rep_count = lax.axis_size("rep")
    slab_index = lax.axis_index("seq")
    rep_index = lax.axis_index("rep")
    query_frames = query_count // frame_rows
    query_blocks = query_count // MASK_BLOCK_SIZE
    score_scale = 1.0 / math.sqrt(HEAD_WIDTH)
    assert rep_count >= 2 and query_frames * rep_count == slab_frames
    assert far_count % rep_count == 0
    far_share = far_count // rep_count

    halo, key_blocks = halo_frame(key_value, key_blocks, frame_rows, seq_count, rep_count, rep_index)
    halo_valid = ((rep_index == 0) & (slab_index > 0)) | (
        (rep_index == rep_count - 1) & (slab_index < seq_count - 1)
    )
    halo = jnp.where(halo_valid, halo, jnp.zeros_like(halo))

    phases = jnp.maximum(key_blocks[0], 0) % FAR_STRIDE
    stride_grid = key_value.reshape(2, far_count, FAR_STRIDE, MASK_BLOCK_SIZE, columns)
    share_grid = lax.dynamic_slice_in_dim(stride_grid, rep_index * far_share, far_share, 1)
    received = []
    pick_list = []
    valid_list = []
    for tier_index in range(LEVELS):
        distance = 2 ** (tier_index + 1)
        if distance >= seq_count:
            continue
        if seq_count <= 2 * distance:
            ahead = [(q, q + distance) for q in range(seq_count - distance)]
            behind = [(q, q - distance) for q in range(distance, seq_count) if q + distance >= seq_count]
            side = (slab_index + distance >= seq_count).astype(jnp.int32)
            slots = [(ahead + behind, side)]
        else:
            ahead = [(q, q + distance) for q in range(seq_count - distance)]
            behind = [(q, q - distance) for q in range(distance, seq_count)]
            slots = [(ahead, jnp.int32(0)), (behind, jnp.int32(1))]
        for pairs, side in slots:
            slot_index = 2 * tier_index + side
            phase = lax.dynamic_index_in_dim(phases, slot_index, 0, keepdims=False)
            wanted = lax.ppermute(phase[None], "seq", pairs)[0]
            chosen = lax.dynamic_index_in_dim(share_grid, wanted, 2, keepdims=False)
            received.append((chosen, [(b, a) for a, b in pairs]))
            partner = slab_index + (1 - 2 * side) * distance
            inside = (partner >= 0) & (partner < seq_count)
            named = lax.dynamic_index_in_dim(key_blocks, slot_index, 1, keepdims=False)
            pick = (named - partner * slab_blocks - phase) // FAR_STRIDE
            pick_list.append(pick)
            valid_list.append((named >= 0) & inside)
    query, payloads = lax.optimization_barrier((query, [chosen for chosen, _ in received]))
    received = [lax.ppermute(chosen, "seq", back) for chosen, (_, back) in zip(payloads, received)]
    slot_count = len(received)

    near = []
    for head in range(head_count):
        cols = slice(head * HEAD_WIDTH, (head + 1) * HEAD_WIDTH)
        query_head = query[:, cols]
        own_scores = (
            jnp.dot(query_head, key_value[0, :, cols].T, preferred_element_type=jnp.float32)
            * score_scale
        )
        halo_scores = (
            jnp.dot(query_head, halo[0, :, cols].T, preferred_element_type=jnp.float32)
            * score_scale
        )
        halo_scores = jnp.where(halo_valid, halo_scores, -jnp.inf)
        near_top = jnp.maximum(
            jnp.max(own_scores, axis=1, keepdims=True), jnp.max(halo_scores, axis=1, keepdims=True)
        )
        own_exp = jnp.exp(own_scores - near_top)
        halo_exp = jnp.exp(halo_scores - near_top)
        near_total = jnp.sum(own_exp, axis=1, keepdims=True) + jnp.sum(
            halo_exp, axis=1, keepdims=True
        )
        near.append((near_top, own_exp, halo_exp, near_total))
    received, near = lax.optimization_barrier((received, near))

    mine = jnp.stack(received, 1)
    parts = [mine]
    sources = [rep_index]
    for k in range(1, rep_count):
        shift = [(r, (r + k) % rep_count) for r in range(rep_count)]
        parts.append(lax.ppermute(mine, "rep", shift))
        sources.append((rep_index - k) % rep_count)
    far_pick = jnp.stack(pick_list, 1)
    far_valid = jnp.stack(valid_list, 1)
    share_ids = jnp.arange(far_share, dtype=jnp.int32)
    far_keys = []
    far_masks = []
    for part, source in zip(parts, sources):
        far_keys.append(part.reshape(2, slot_count * far_share * MASK_BLOCK_SIZE, columns))
        named = source * far_share + share_ids
        mask = far_valid[:, :, None] & (far_pick[:, :, None] == named[None, None, :])
        mask = mask.reshape(query_blocks, 1, slot_count * far_share)
        far_masks.append(jnp.repeat(mask, MASK_BLOCK_SIZE, axis=2))

    outputs = []
    for head in range(head_count):
        cols = slice(head * HEAD_WIDTH, (head + 1) * HEAD_WIDTH)
        near_top, own_exp, halo_exp, near_total = near[head]
        row_top = near_top
        far_scores = []
        for keys, mask in zip(far_keys, far_masks):
            scores = (
                jnp.dot(query[:, cols], keys[0, :, cols].T, preferred_element_type=jnp.float32)
                * score_scale
            )
            scores = jnp.where(
                mask, scores.reshape(query_blocks, MASK_BLOCK_SIZE, -1), -jnp.inf
            ).reshape(query_count, -1)
            far_scores.append(scores)
            row_top = jnp.maximum(row_top, jnp.max(scores, axis=1, keepdims=True))
        near_factor = jnp.exp(near_top - row_top)
        far_exp = [jnp.exp(scores - row_top) for scores in far_scores]
        row_total = near_total * near_factor
        for part_exp in far_exp:
            row_total = row_total + jnp.sum(part_exp, axis=1, keepdims=True)
        near_scale = near_factor / row_total
        own_prob = (own_exp * near_scale).astype(jnp.bfloat16)
        halo_prob = (halo_exp * near_scale).astype(jnp.bfloat16)
        mixed = jnp.dot(own_prob, key_value[1, :, cols], preferred_element_type=jnp.float32)
        mixed = mixed + jnp.dot(halo_prob, halo[1, :, cols], preferred_element_type=jnp.float32)
        for part_exp, keys in zip(far_exp, far_keys):
            part_prob = (part_exp / row_total).astype(jnp.bfloat16)
            mixed = mixed + jnp.dot(part_prob, keys[1, :, cols], preferred_element_type=jnp.float32)
        outputs.append(mixed.astype(jnp.bfloat16))
    return jnp.stack(outputs, axis=1).reshape(query_count, columns)


def solution(mesh):
    in_specs = (
        P(("grp", "seq", "rep"), "head"),
        P(None, ("grp", "seq"), "head"),
        P(("grp", "seq", "rep"), None),
    )
    out_specs = P(("grp", "seq", "rep"), "head")
    return jax.shard_map(
        per_device, mesh=mesh, in_specs=in_specs, out_specs=out_specs, check_vma=False
    )
```

```python
import math

import jax
import jax.numpy as jnp
from jax import lax
from jax.sharding import PartitionSpec as P

HEAD_WIDTH = 128
MASK_BLOCK_SIZE = 128
BLOCKS_PER_FRAME = 4
FAR_STRIDE = 4
LEVELS = 4


def from_behind(shard, axis, by):
    count = lax.axis_size(axis)
    pairs = [(i, i + by) for i in range(count) if 0 <= i + by < count]
    return lax.ppermute(shard, axis, pairs)


def halo_frame(key_value, key_blocks, frame_rows, seq_count, rep_count, rep_index):
    slab_rows = key_value.shape[1]
    start = jnp.where(rep_index == rep_count - 1, slab_rows - frame_rows, 0)
    payload = lax.dynamic_slice_in_dim(key_value, start, frame_rows, 1)
    key_blocks, payload = lax.optimization_barrier((key_blocks, payload))
    pairs = [(s * rep_count + rep_count - 1, (s + 1) * rep_count) for s in range(seq_count - 1)]
    pairs += [(s * rep_count, (s - 1) * rep_count + rep_count - 1) for s in range(1, seq_count)]
    return lax.ppermute(payload, ("seq", "rep"), pairs), key_blocks


def per_device(query, key_value, key_blocks):
    frame_rows = BLOCKS_PER_FRAME * MASK_BLOCK_SIZE
    query_count = query.shape[0]
    slab_rows = key_value.shape[1]
    columns = key_value.shape[2]
    head_count = columns // HEAD_WIDTH
    slab_blocks = slab_rows // MASK_BLOCK_SIZE
    slab_frames = slab_rows // frame_rows
    far_count = slab_blocks // FAR_STRIDE
    seq_count = lax.axis_size("seq")
    rep_count = lax.axis_size("rep")
    slab_index = lax.axis_index("seq")
    rep_index = lax.axis_index("rep")
    query_frames = query_count // frame_rows
    query_blocks = query_count // MASK_BLOCK_SIZE
    score_scale = 1.0 / math.sqrt(HEAD_WIDTH)
    assert rep_count >= 2 and query_frames * rep_count == slab_frames
    assert far_count % rep_count == 0
    far_share = far_count // rep_count

    halo, key_blocks = halo_frame(key_value, key_blocks, frame_rows, seq_count, rep_count, rep_index)
    halo_valid = ((rep_index == 0) & (slab_index > 0)) | (
        (rep_index == rep_count - 1) & (slab_index < seq_count - 1)
    )
    halo = jnp.where(halo_valid, halo, jnp.zeros_like(halo))

    phases = jnp.maximum(key_blocks[0], 0) % FAR_STRIDE
    stride_grid = key_value.reshape(2, far_count, FAR_STRIDE, MASK_BLOCK_SIZE, columns)
    share_grid = lax.dynamic_slice_in_dim(stride_grid, rep_index * far_share, far_share, 1)
    received = []
    pick_list = []
    valid_list = []
    for tier_index in range(LEVELS):
        distance = 2 ** (tier_index + 1)
        if distance >= seq_count:
            continue
        if seq_count <= 2 * distance:
            ahead = [(q, q + distance) for q in range(seq_count - distance)]
            behind = [(q, q - distance) for q in range(distance, seq_count) if q + distance >= seq_count]
            side = (slab_index + distance >= seq_count).astype(jnp.int32)
            slots = [(ahead + behind, side)]
        else:
            ahead = [(q, q + distance) for q in range(seq_count - distance)]
            behind = [(q, q - distance) for q in range(distance, seq_count)]
            slots = [(ahead, jnp.int32(0)), (behind, jnp.int32(1))]
        for pairs, side in slots:
            slot_index = 2 * tier_index + side
            phase = lax.dynamic_index_in_dim(phases, slot_index, 0, keepdims=False)
            wanted = lax.ppermute(phase[None], "seq", pairs)[0]
            chosen = lax.dynamic_index_in_dim(share_grid, wanted, 2, keepdims=False)
            received.append((chosen, [(b, a) for a, b in pairs]))
            partner = slab_index + (1 - 2 * side) * distance
            inside = (partner >= 0) & (partner < seq_count)
            named = lax.dynamic_index_in_dim(key_blocks, slot_index, 1, keepdims=False)
            pick = (named - partner * slab_blocks - phase) // FAR_STRIDE
            pick_list.append(pick)
            valid_list.append((named >= 0) & inside)
    query, payloads = lax.optimization_barrier((query, [chosen for chosen, _ in received]))
    received = [
        jnp.stack([lax.ppermute(chosen[i], "seq", back) for i in range(2)])
        for chosen, (_, back) in zip(payloads, received)
    ]
    slot_count = len(received)

    near = []
    for head in range(head_count):
        cols = slice(head * HEAD_WIDTH, (head + 1) * HEAD_WIDTH)
        query_head = query[:, cols]
        own_scores = (
            jnp.dot(query_head, key_value[0, :, cols].T, preferred_element_type=jnp.float32)
            * score_scale
        )
        halo_scores = (
            jnp.dot(query_head, halo[0, :, cols].T, preferred_element_type=jnp.float32)
            * score_scale
        )
        halo_scores = jnp.where(halo_valid, halo_scores, -jnp.inf)
        near_top = jnp.maximum(
            jnp.max(own_scores, axis=1, keepdims=True), jnp.max(halo_scores, axis=1, keepdims=True)
        )
        own_exp = jnp.exp(own_scores - near_top)
        halo_exp = jnp.exp(halo_scores - near_top)
        near_total = jnp.sum(own_exp, axis=1, keepdims=True) + jnp.sum(
            halo_exp, axis=1, keepdims=True
        )
        near.append((near_top, own_exp, halo_exp, near_total))
    received, near = lax.optimization_barrier((received, near))

    mine = jnp.stack(received, 1)
    parts = [mine]
    sources = [rep_index]
    for k in range(1, rep_count):
        shift = [(r, (r + k) % rep_count) for r in range(rep_count)]
        parts.append(lax.ppermute(mine, "rep", shift))
        sources.append((rep_index - k) % rep_count)
    far_pair = jnp.stack(parts, 2).reshape(2, slot_count * far_count * MASK_BLOCK_SIZE, columns)
    far_pick = jnp.stack(pick_list, 1)
    far_valid = jnp.stack(valid_list, 1)
    share_ids = jnp.arange(far_share, dtype=jnp.int32)
    candidates = (jnp.stack(sources)[:, None] * far_share + share_ids[None, :]).reshape(far_count)
    far_mask = far_valid[:, :, None] & (far_pick[:, :, None] == candidates[None, None, :])
    far_mask = jnp.repeat(far_mask.reshape(query_blocks, 1, slot_count * far_count), MASK_BLOCK_SIZE, axis=2)

    outputs = []
    for head in range(head_count):
        cols = slice(head * HEAD_WIDTH, (head + 1) * HEAD_WIDTH)
        near_top, own_exp, halo_exp, near_total = near[head]
        far_scores = (
            jnp.dot(query[:, cols], far_pair[0, :, cols].T, preferred_element_type=jnp.float32)
            * score_scale
        )
        far_scores = jnp.where(
            far_mask, far_scores.reshape(query_blocks, MASK_BLOCK_SIZE, -1), -jnp.inf
        ).reshape(query_count, -1)
        row_top = jnp.maximum(near_top, jnp.max(far_scores, axis=1, keepdims=True))
        near_factor = jnp.exp(near_top - row_top)
        far_exp = jnp.exp(far_scores - row_top)
        row_total = near_total * near_factor + jnp.sum(far_exp, axis=1, keepdims=True)
        near_scale = near_factor / row_total
        own_prob = (own_exp * near_scale).astype(jnp.bfloat16)
        halo_prob = (halo_exp * near_scale).astype(jnp.bfloat16)
        far_prob = (far_exp / row_total).astype(jnp.bfloat16)
        mixed = jnp.dot(own_prob, key_value[1, :, cols], preferred_element_type=jnp.float32)
        mixed = mixed + jnp.dot(halo_prob, halo[1, :, cols], preferred_element_type=jnp.float32)
        mixed = mixed + jnp.dot(far_prob, far_pair[1, :, cols], preferred_element_type=jnp.float32)
        outputs.append(mixed.astype(jnp.bfloat16))
    return jnp.concatenate(outputs, axis=1)


def solution(mesh):
    in_specs = (
        P(("grp", "seq", "rep"), "head"),
        P(None, ("grp", "seq"), "head"),
        P(("grp", "seq", "rep"), None),
    )
    out_specs = P(("grp", "seq", "rep"), "head")
    return jax.shard_map(
        per_device, mesh=mesh, in_specs=in_specs, out_specs=out_specs, check_vma=False
    )
```

```python
import math

import jax
import jax.numpy as jnp
from jax import lax
from jax.sharding import PartitionSpec as P

HEAD_WIDTH = 128
MASK_BLOCK_SIZE = 128
BLOCKS_PER_FRAME = 4
FAR_STRIDE = 4
LEVELS = 4


def from_behind(shard, axis, by):
    count = lax.axis_size(axis)
    pairs = [(i, i + by) for i in range(count) if 0 <= i + by < count]
    return lax.ppermute(shard, axis, pairs)


def halo_frame(key_value, key_blocks, frame_rows, seq_count, rep_count, rep_index):
    slab_rows = key_value.shape[1]
    start = jnp.where(rep_index == rep_count - 1, slab_rows - frame_rows, 0)
    payload = lax.dynamic_slice_in_dim(key_value, start, frame_rows, 1)
    key_blocks, payload = lax.optimization_barrier((key_blocks, payload))
    pairs = [(s * rep_count + rep_count - 1, (s + 1) * rep_count) for s in range(seq_count - 1)]
    pairs += [(s * rep_count, (s - 1) * rep_count + rep_count - 1) for s in range(1, seq_count)]
    return lax.ppermute(payload, ("seq", "rep"), pairs), key_blocks


def per_device(query, key_value, key_blocks):
    frame_rows = BLOCKS_PER_FRAME * MASK_BLOCK_SIZE
    query_count = query.shape[0]
    slab_rows = key_value.shape[1]
    columns = key_value.shape[2]
    head_count = columns // HEAD_WIDTH
    slab_blocks = slab_rows // MASK_BLOCK_SIZE
    slab_frames = slab_rows // frame_rows
    far_count = slab_blocks // FAR_STRIDE
    seq_count = lax.axis_size("seq")
    rep_count = lax.axis_size("rep")
    slab_index = lax.axis_index("seq")
    rep_index = lax.axis_index("rep")
    query_frames = query_count // frame_rows
    query_blocks = query_count // MASK_BLOCK_SIZE
    score_scale = 1.0 / math.sqrt(HEAD_WIDTH)
    assert rep_count >= 2 and query_frames * rep_count == slab_frames
    assert far_count % rep_count == 0
    far_share = far_count // rep_count

    halo, key_blocks = halo_frame(key_value, key_blocks, frame_rows, seq_count, rep_count, rep_index)
    halo_valid = ((rep_index == 0) & (slab_index > 0)) | (
        (rep_index == rep_count - 1) & (slab_index < seq_count - 1)
    )
    halo = jnp.where(halo_valid, halo, jnp.zeros_like(halo))

    phases = jnp.maximum(key_blocks[0], 0) % FAR_STRIDE
    stride_grid = key_value.reshape(2, far_count, FAR_STRIDE, MASK_BLOCK_SIZE, columns)
    share_grid = lax.dynamic_slice_in_dim(stride_grid, rep_index * far_share, far_share, 1)
    received = []
    pick_list = []
    valid_list = []
    for tier_index in range(LEVELS):
        distance = 2 ** (tier_index + 1)
        if distance >= seq_count:
            continue
        if seq_count <= 2 * distance:
            ahead = [(q, q + distance) for q in range(seq_count - distance)]
            behind = [(q, q - distance) for q in range(distance, seq_count) if q + distance >= seq_count]
            side = (slab_index + distance >= seq_count).astype(jnp.int32)
            slots = [(ahead + behind, side)]
        else:
            ahead = [(q, q + distance) for q in range(seq_count - distance)]
            behind = [(q, q - distance) for q in range(distance, seq_count)]
            slots = [(ahead, jnp.int32(0)), (behind, jnp.int32(1))]
        for pairs, side in slots:
            slot_index = 2 * tier_index + side
            phase = lax.dynamic_index_in_dim(phases, slot_index, 0, keepdims=False)
            wanted = lax.ppermute(phase[None], "seq", pairs)[0]
            chosen = lax.dynamic_index_in_dim(share_grid, wanted, 2, keepdims=False)
            received.append((chosen, [(b, a) for a, b in pairs]))
            partner = slab_index + (1 - 2 * side) * distance
            inside = (partner >= 0) & (partner < seq_count)
            named = lax.dynamic_index_in_dim(key_blocks, slot_index, 1, keepdims=False)
            pick = (named - partner * slab_blocks - phase) // FAR_STRIDE
            pick_list.append(pick)
            valid_list.append((named >= 0) & inside)
    query, payloads = lax.optimization_barrier((query, [chosen for chosen, _ in received]))
    backs = [back for _, back in received]
    received = [lax.ppermute(chosen[0][None], "seq", back) for chosen, back in zip(payloads, backs)]
    later_values = [chosen[1][None] for chosen in payloads]
    slot_count = len(received)

    near = []
    for head in range(head_count):
        cols = slice(head * HEAD_WIDTH, (head + 1) * HEAD_WIDTH)
        query_head = query[:, cols]
        own_scores = (
            jnp.dot(query_head, key_value[0, :, cols].T, preferred_element_type=jnp.float32)
            * score_scale
        )
        halo_scores = (
            jnp.dot(query_head, halo[0, :, cols].T, preferred_element_type=jnp.float32)
            * score_scale
        )
        halo_scores = jnp.where(halo_valid, halo_scores, -jnp.inf)
        near_top = jnp.maximum(
            jnp.max(own_scores, axis=1, keepdims=True), jnp.max(halo_scores, axis=1, keepdims=True)
        )
        own_exp = jnp.exp(own_scores - near_top)
        halo_exp = jnp.exp(halo_scores - near_top)
        near_total = jnp.sum(own_exp, axis=1, keepdims=True) + jnp.sum(
            halo_exp, axis=1, keepdims=True
        )
        near.append((near_top, own_exp, halo_exp, near_total))
    received, near, later_values = lax.optimization_barrier((received, near, later_values))
    values = [lax.ppermute(chosen, "seq", back) for chosen, back in zip(later_values, backs)]

    def gather_reps(pieces):
        mine = jnp.stack(pieces, 1)
        parts = [mine]
        for k in range(1, rep_count):
            shift = [(r, (r + k) % rep_count) for r in range(rep_count)]
            parts.append(lax.ppermute(mine, "rep", shift))
        return jnp.stack(parts, 2).reshape(slot_count * far_count * MASK_BLOCK_SIZE, columns)

    sources = [(rep_index - k) % rep_count for k in range(rep_count)]
    far_keys = gather_reps(received)
    far_pick = jnp.stack(pick_list, 1)
    far_valid = jnp.stack(valid_list, 1)
    share_ids = jnp.arange(far_share, dtype=jnp.int32)
    candidates = (jnp.stack(sources)[:, None] * far_share + share_ids[None, :]).reshape(far_count)
    far_mask = far_valid[:, :, None] & (far_pick[:, :, None] == candidates[None, None, :])
    far_mask = jnp.repeat(far_mask.reshape(query_blocks, 1, slot_count * far_count), MASK_BLOCK_SIZE, axis=2)

    outputs = []
    for head in range(head_count):
        cols = slice(head * HEAD_WIDTH, (head + 1) * HEAD_WIDTH)
        near_top, own_exp, halo_exp, near_total = near[head]
        far_scores = (
            jnp.dot(query[:, cols], far_keys[:, cols].T, preferred_element_type=jnp.float32)
            * score_scale
        )
        far_scores = jnp.where(
            far_mask, far_scores.reshape(query_blocks, MASK_BLOCK_SIZE, -1), -jnp.inf
        ).reshape(query_count, -1)
        row_top = jnp.maximum(near_top, jnp.max(far_scores, axis=1, keepdims=True))
        near_factor = jnp.exp(near_top - row_top)
        far_exp = jnp.exp(far_scores - row_top)
        row_total = near_total * near_factor + jnp.sum(far_exp, axis=1, keepdims=True)
        near_scale = near_factor / row_total
        own_prob = (own_exp * near_scale).astype(jnp.bfloat16)
        halo_prob = (halo_exp * near_scale).astype(jnp.bfloat16)
        far_prob = (far_exp / row_total).astype(jnp.bfloat16)
        mixed = jnp.dot(own_prob, key_value[1, :, cols], preferred_element_type=jnp.float32)
        mixed = mixed + jnp.dot(halo_prob, halo[1, :, cols], preferred_element_type=jnp.float32)
        outputs.append((mixed, far_prob))
    values, outputs = lax.optimization_barrier((values, outputs))
    far_values = gather_reps(values)
    finished = []
    for head, (mixed, far_prob) in enumerate(outputs):
        cols = slice(head * HEAD_WIDTH, (head + 1) * HEAD_WIDTH)
        mixed = mixed + jnp.dot(far_prob, far_values[:, cols], preferred_element_type=jnp.float32)
        finished.append(mixed.astype(jnp.bfloat16))
    return jnp.concatenate(finished, axis=1)


def solution(mesh):
    in_specs = (
        P(("grp", "seq", "rep"), "head"),
        P(None, ("grp", "seq"), "head"),
        P(("grp", "seq", "rep"), None),
    )
    out_specs = P(("grp", "seq", "rep"), "head")
    return jax.shard_map(
        per_device, mesh=mesh, in_specs=in_specs, out_specs=out_specs, check_vma=False
    )
```

```python
import math

import jax
import jax.numpy as jnp
from jax import lax
from jax.sharding import PartitionSpec as P

HEAD_WIDTH = 128
MASK_BLOCK_SIZE = 128
BLOCKS_PER_FRAME = 4
FAR_STRIDE = 4
LEVELS = 4


def from_behind(shard, axis, by):
    count = lax.axis_size(axis)
    pairs = [(i, i + by) for i in range(count) if 0 <= i + by < count]
    return lax.ppermute(shard, axis, pairs)


def halo_frame(key_value, key_blocks, frame_rows, seq_count, rep_count, rep_index):
    slab_rows = key_value.shape[1]
    start = jnp.where(rep_index == rep_count - 1, slab_rows - frame_rows, 0)
    payload = lax.dynamic_slice_in_dim(key_value, start, frame_rows, 1)
    key_blocks, payload = lax.optimization_barrier((key_blocks, payload))
    pairs = [(s * rep_count + rep_count - 1, (s + 1) * rep_count) for s in range(seq_count - 1)]
    pairs += [(s * rep_count, (s - 1) * rep_count + rep_count - 1) for s in range(1, seq_count)]
    return lax.ppermute(payload, ("seq", "rep"), pairs), key_blocks


def per_device(query, key_value, key_blocks):
    frame_rows = BLOCKS_PER_FRAME * MASK_BLOCK_SIZE
    query_count = query.shape[0]
    slab_rows = key_value.shape[1]
    columns = key_value.shape[2]
    head_count = columns // HEAD_WIDTH
    slab_blocks = slab_rows // MASK_BLOCK_SIZE
    slab_frames = slab_rows // frame_rows
    far_count = slab_blocks // FAR_STRIDE
    seq_count = lax.axis_size("seq")
    rep_count = lax.axis_size("rep")
    slab_index = lax.axis_index("seq")
    rep_index = lax.axis_index("rep")
    query_frames = query_count // frame_rows
    query_blocks = query_count // MASK_BLOCK_SIZE
    score_scale = 1.0 / math.sqrt(HEAD_WIDTH)
    assert rep_count >= 2 and query_frames * rep_count == slab_frames
    assert far_count % rep_count == 0
    far_share = far_count // rep_count

    halo, key_blocks = halo_frame(key_value, key_blocks, frame_rows, seq_count, rep_count, rep_index)
    halo_valid = ((rep_index == 0) & (slab_index > 0)) | (
        (rep_index == rep_count - 1) & (slab_index < seq_count - 1)
    )
    halo = jnp.where(halo_valid, halo, jnp.zeros_like(halo))

    phases = jnp.maximum(key_blocks[0], 0) % FAR_STRIDE
    stride_grid = key_value.reshape(2, far_count, FAR_STRIDE, MASK_BLOCK_SIZE, columns)
    share_grid = lax.dynamic_slice_in_dim(stride_grid, rep_index * far_share, far_share, 1)
    received = []
    pick_list = []
    valid_list = []
    for tier_index in range(LEVELS):
        distance = 2 ** (tier_index + 1)
        if distance >= seq_count:
            continue
        if seq_count <= 2 * distance:
            ahead = [(q, q + distance) for q in range(seq_count - distance)]
            behind = [(q, q - distance) for q in range(distance, seq_count) if q + distance >= seq_count]
            side = (slab_index + distance >= seq_count).astype(jnp.int32)
            slots = [(ahead + behind, side)]
        else:
            ahead = [(q, q + distance) for q in range(seq_count - distance)]
            behind = [(q, q - distance) for q in range(distance, seq_count)]
            slots = [(ahead, jnp.int32(0)), (behind, jnp.int32(1))]
        for pairs, side in slots:
            slot_index = 2 * tier_index + side
            phase = lax.dynamic_index_in_dim(phases, slot_index, 0, keepdims=False)
            wanted = lax.ppermute(phase[None], "seq", pairs)[0]
            chosen = lax.dynamic_index_in_dim(share_grid, wanted, 2, keepdims=False)
            received.append((chosen, [(b, a) for a, b in pairs]))
            partner = slab_index + (1 - 2 * side) * distance
            inside = (partner >= 0) & (partner < seq_count)
            named = lax.dynamic_index_in_dim(key_blocks, slot_index, 1, keepdims=False)
            pick = (named - partner * slab_blocks - phase) // FAR_STRIDE
            pick_list.append(pick)
            valid_list.append((named >= 0) & inside)
    query, payloads = lax.optimization_barrier((query, [chosen for chosen, _ in received]))
    backs = [back for _, back in received]
    received = [lax.ppermute(chosen[0][None], "seq", back) for chosen, back in zip(payloads, backs)]
    later_values = [chosen[1][None] for chosen in payloads]
    slot_count = len(received)

    near = []
    for head in range(head_count):
        cols = slice(head * HEAD_WIDTH, (head + 1) * HEAD_WIDTH)
        query_head = query[:, cols]
        own_scores = (
            jnp.dot(query_head, key_value[0, :, cols].T, preferred_element_type=jnp.float32)
            * score_scale
        )
        halo_scores = (
            jnp.dot(query_head, halo[0, :, cols].T, preferred_element_type=jnp.float32)
            * score_scale
        )
        halo_scores = jnp.where(halo_valid, halo_scores, -jnp.inf)
        near_top = jnp.maximum(
            jnp.max(own_scores, axis=1, keepdims=True), jnp.max(halo_scores, axis=1, keepdims=True)
        )
        own_exp = jnp.exp(own_scores - near_top)
        halo_exp = jnp.exp(halo_scores - near_top)
        near_total = jnp.sum(own_exp, axis=1, keepdims=True) + jnp.sum(
            halo_exp, axis=1, keepdims=True
        )
        near.append((near_top, own_exp, halo_exp, near_total))
    received, near, later_values = lax.optimization_barrier((received, near, later_values))
    values = [lax.ppermute(chosen, "seq", back) for chosen, back in zip(later_values, backs)]

    def gather_reps(pieces):
        mine = jnp.stack(pieces, 1)
        parts = [mine]
        for k in range(1, rep_count):
            shift = [(r, (r + k) % rep_count) for r in range(rep_count)]
            parts.append(lax.ppermute(mine, "rep", shift))
        return jnp.stack(parts, 2).reshape(slot_count * far_count * MASK_BLOCK_SIZE, columns)

    sources = [(rep_index - k) % rep_count for k in range(rep_count)]
    far_keys = gather_reps(received)
    far_pick = jnp.stack(pick_list, 1)
    far_valid = jnp.stack(valid_list, 1)
    share_ids = jnp.arange(far_share, dtype=jnp.int32)
    candidates = (jnp.stack(sources)[:, None] * far_share + share_ids[None, :]).reshape(far_count)
    far_mask = far_valid[:, :, None] & (far_pick[:, :, None] == candidates[None, None, :])
    far_mask = jnp.repeat(far_mask.reshape(query_blocks, 1, slot_count * far_count), MASK_BLOCK_SIZE, axis=2)

    outputs = []
    for head in range(head_count):
        cols = slice(head * HEAD_WIDTH, (head + 1) * HEAD_WIDTH)
        near_top, own_exp, halo_exp, near_total = near[head]
        far_scores = (
            jnp.dot(query[:, cols], far_keys[:, cols].T, preferred_element_type=jnp.float32)
            * score_scale
        )
        far_scores = jnp.where(
            far_mask, far_scores.reshape(query_blocks, MASK_BLOCK_SIZE, -1), -jnp.inf
        ).reshape(query_count, -1)
        row_top = jnp.maximum(near_top, jnp.max(far_scores, axis=1, keepdims=True))
        near_factor = jnp.exp(near_top - row_top)
        far_exp = jnp.exp(far_scores - row_top)
        row_total = near_total * near_factor + jnp.sum(far_exp, axis=1, keepdims=True)
        near_scale = near_factor / row_total
        own_prob = (own_exp * near_scale).astype(jnp.bfloat16)
        halo_prob = (halo_exp * near_scale).astype(jnp.bfloat16)
        far_prob = (far_exp / row_total).astype(jnp.bfloat16)
        mixed = jnp.dot(own_prob, key_value[1, :, cols], preferred_element_type=jnp.float32)
        mixed = mixed + jnp.dot(halo_prob, halo[1, :, cols], preferred_element_type=jnp.float32)
        outputs.append((mixed, far_prob))
    values, outputs = lax.optimization_barrier((values, outputs))
    far_values = gather_reps(values)
    near_part = jnp.stack([mixed for mixed, _ in outputs], axis=1)
    far_probs = jnp.stack([far_prob for _, far_prob in outputs], axis=0)
    far_part = jnp.einsum(
        "hqk,khd->qhd",
        far_probs,
        far_values.reshape(-1, head_count, HEAD_WIDTH),
        preferred_element_type=jnp.float32,
    )
    return (near_part + far_part).astype(jnp.bfloat16).reshape(query_count, columns)


def solution(mesh):
    in_specs = (
        P(("grp", "seq", "rep"), "head"),
        P(None, ("grp", "seq"), "head"),
        P(("grp", "seq", "rep"), None),
    )
    out_specs = P(("grp", "seq", "rep"), "head")
    return jax.shard_map(
        per_device, mesh=mesh, in_specs=in_specs, out_specs=out_specs, check_vma=False
    )
```

```python
import math

import jax
import jax.numpy as jnp
from jax import lax
from jax.sharding import PartitionSpec as P

HEAD_WIDTH = 128
MASK_BLOCK_SIZE = 128
BLOCKS_PER_FRAME = 4
FAR_STRIDE = 4
LEVELS = 4


def from_behind(shard, axis, by):
    count = lax.axis_size(axis)
    pairs = [(i, i + by) for i in range(count) if 0 <= i + by < count]
    return lax.ppermute(shard, axis, pairs)


def halo_frame(key_value, key_blocks, frame_rows, seq_count, rep_count, rep_index):
    slab_rows = key_value.shape[1]
    start = jnp.where(rep_index == rep_count - 1, slab_rows - frame_rows, 0)
    payload = lax.dynamic_slice_in_dim(key_value, start, frame_rows, 1)
    key_blocks, payload = lax.optimization_barrier((key_blocks, payload))
    pairs = [(s * rep_count + rep_count - 1, (s + 1) * rep_count) for s in range(seq_count - 1)]
    pairs += [(s * rep_count, (s - 1) * rep_count + rep_count - 1) for s in range(1, seq_count)]
    return lax.ppermute(payload, ("seq", "rep"), pairs), key_blocks


def per_device(query, key_value, key_blocks):
    frame_rows = BLOCKS_PER_FRAME * MASK_BLOCK_SIZE
    query_count = query.shape[0]
    slab_rows = key_value.shape[1]
    columns = key_value.shape[2]
    head_count = columns // HEAD_WIDTH
    slab_blocks = slab_rows // MASK_BLOCK_SIZE
    slab_frames = slab_rows // frame_rows
    far_count = slab_blocks // FAR_STRIDE
    seq_count = lax.axis_size("seq")
    rep_count = lax.axis_size("rep")
    slab_index = lax.axis_index("seq")
    rep_index = lax.axis_index("rep")
    query_frames = query_count // frame_rows
    query_blocks = query_count // MASK_BLOCK_SIZE
    score_scale = 1.0 / math.sqrt(HEAD_WIDTH)
    assert rep_count >= 2 and query_frames * rep_count == slab_frames
    assert far_count % rep_count == 0
    far_share = far_count // rep_count

    halo, key_blocks = halo_frame(key_value, key_blocks, frame_rows, seq_count, rep_count, rep_index)
    halo_valid = ((rep_index == 0) & (slab_index > 0)) | (
        (rep_index == rep_count - 1) & (slab_index < seq_count - 1)
    )
    halo = jnp.where(halo_valid, halo, jnp.zeros_like(halo))

    phases = jnp.maximum(key_blocks[0], 0) % FAR_STRIDE
    stride_grid = key_value.reshape(2, far_count, FAR_STRIDE, MASK_BLOCK_SIZE, columns)
    share_grid = lax.dynamic_slice_in_dim(stride_grid, rep_index * far_share, far_share, 1)
    received = []
    pick_list = []
    valid_list = []
    for tier_index in range(LEVELS):
        distance = 2 ** (tier_index + 1)
        if distance >= seq_count:
            continue
        if seq_count <= 2 * distance:
            ahead = [(q, q + distance) for q in range(seq_count - distance)]
            behind = [(q, q - distance) for q in range(distance, seq_count) if q + distance >= seq_count]
            side = (slab_index + distance >= seq_count).astype(jnp.int32)
            slots = [(ahead + behind, side)]
        else:
            ahead = [(q, q + distance) for q in range(seq_count - distance)]
            behind = [(q, q - distance) for q in range(distance, seq_count)]
            slots = [(ahead, jnp.int32(0)), (behind, jnp.int32(1))]
        for pairs, side in slots:
            slot_index = 2 * tier_index + side
            phase = lax.dynamic_index_in_dim(phases, slot_index, 0, keepdims=False)
            wanted = lax.ppermute(phase[None], "seq", pairs)[0]
            chosen = lax.dynamic_index_in_dim(share_grid, wanted, 2, keepdims=False)
            received.append((chosen, [(b, a) for a, b in pairs]))
            partner = slab_index + (1 - 2 * side) * distance
            inside = (partner >= 0) & (partner < seq_count)
            named = lax.dynamic_index_in_dim(key_blocks, slot_index, 1, keepdims=False)
            pick = (named - partner * slab_blocks - phase) // FAR_STRIDE
            pick_list.append(pick)
            valid_list.append((named >= 0) & inside)
    query, payloads = lax.optimization_barrier((query, [chosen for chosen, _ in received]))
    backs = [back for _, back in received]
    received = [lax.ppermute(chosen[0][None], "seq", back) for chosen, back in zip(payloads, backs)]
    later_values = [chosen[1][None] for chosen in payloads]
    slot_count = len(received)

    near = []
    for head in range(head_count):
        cols = slice(head * HEAD_WIDTH, (head + 1) * HEAD_WIDTH)
        query_head = query[:, cols]
        own_scores = (
            jnp.dot(query_head, key_value[0, :, cols].T, preferred_element_type=jnp.float32)
            * score_scale
        )
        halo_scores = (
            jnp.dot(query_head, halo[0, :, cols].T, preferred_element_type=jnp.float32)
            * score_scale
        )
        halo_scores = jnp.where(halo_valid, halo_scores, -jnp.inf)
        near_top = jnp.maximum(
            jnp.max(own_scores, axis=1, keepdims=True), jnp.max(halo_scores, axis=1, keepdims=True)
        )
        own_exp = jnp.exp(own_scores - near_top)
        halo_exp = jnp.exp(halo_scores - near_top)
        near_total = jnp.sum(own_exp, axis=1, keepdims=True) + jnp.sum(
            halo_exp, axis=1, keepdims=True
        )
        near.append((near_top, own_exp, halo_exp, near_total))
    received, near, later_values = lax.optimization_barrier((received, near, later_values))
    values = [lax.ppermute(chosen, "seq", back) for chosen, back in zip(later_values, backs)]

    def gather_reps(pieces):
        mine = jnp.stack(pieces, 1)
        parts = [mine]
        for k in range(1, rep_count):
            shift = [(r, (r + k) % rep_count) for r in range(rep_count)]
            parts.append(lax.ppermute(mine, "rep", shift))
        return jnp.stack(parts, 2).reshape(slot_count * far_count * MASK_BLOCK_SIZE, columns)

    sources = [(rep_index - k) % rep_count for k in range(rep_count)]
    far_keys = gather_reps(received)
    far_pick = jnp.stack(pick_list, 1)
    far_valid = jnp.stack(valid_list, 1)
    share_ids = jnp.arange(far_share, dtype=jnp.int32)
    candidates = (jnp.stack(sources)[:, None] * far_share + share_ids[None, :]).reshape(far_count)
    far_mask = far_valid[:, :, None] & (far_pick[:, :, None] == candidates[None, None, :])
    far_mask = jnp.repeat(far_mask.reshape(query_blocks, 1, slot_count * far_count), MASK_BLOCK_SIZE, axis=2)

    outputs = []
    for head in range(head_count):
        cols = slice(head * HEAD_WIDTH, (head + 1) * HEAD_WIDTH)
        near_top, own_exp, halo_exp, near_total = near[head]
        far_scores = (
            jnp.dot(query[:, cols], far_keys[:, cols].T, preferred_element_type=jnp.float32)
            * score_scale
        )
        far_scores = jnp.where(
            far_mask, far_scores.reshape(query_blocks, MASK_BLOCK_SIZE, -1), -jnp.inf
        ).reshape(query_count, -1)
        row_top = jnp.maximum(near_top, jnp.max(far_scores, axis=1, keepdims=True))
        near_factor = jnp.exp(near_top - row_top)
        far_exp = jnp.exp(far_scores - row_top)
        row_total = near_total * near_factor + jnp.sum(far_exp, axis=1, keepdims=True)
        near_scale = near_factor / row_total
        own_prob = (own_exp * near_scale).astype(jnp.bfloat16)
        halo_prob = (halo_exp * near_scale).astype(jnp.bfloat16)
        far_prob = (far_exp / row_total).astype(jnp.bfloat16)
        mixed = jnp.dot(own_prob, key_value[1, :, cols], preferred_element_type=jnp.float32)
        mixed = mixed + jnp.dot(halo_prob, halo[1, :, cols], preferred_element_type=jnp.float32)
        outputs.append((mixed, far_prob))
    values, outputs = lax.optimization_barrier((values, outputs))
    mine = jnp.stack(values, 1)
    value_parts = [mine]
    for k in range(1, rep_count):
        shift = [(r, (r + k) % rep_count) for r in range(rep_count)]
        value_parts.append(lax.ppermute(mine, "rep", shift))
    part_rows = slot_count * far_share * MASK_BLOCK_SIZE
    value_parts = [part.reshape(part_rows, columns) for part in value_parts]
    finished = []
    for head, (mixed, far_prob) in enumerate(outputs):
        cols = slice(head * HEAD_WIDTH, (head + 1) * HEAD_WIDTH)
        far_prob = far_prob.reshape(query_count, slot_count, rep_count, far_share * MASK_BLOCK_SIZE)
        for k, part in enumerate(value_parts):
            part_prob = far_prob[:, :, k].reshape(query_count, part_rows)
            mixed = mixed + jnp.dot(part_prob, part[:, cols], preferred_element_type=jnp.float32)
        finished.append(mixed.astype(jnp.bfloat16))
    return jnp.concatenate(finished, axis=1)


def solution(mesh):
    in_specs = (
        P(("grp", "seq", "rep"), "head"),
        P(None, ("grp", "seq"), "head"),
        P(("grp", "seq", "rep"), None),
    )
    out_specs = P(("grp", "seq", "rep"), "head")
    return jax.shard_map(
        per_device, mesh=mesh, in_specs=in_specs, out_specs=out_specs, check_vma=False
    )
```

```python
import math

import jax
import jax.numpy as jnp
from jax import lax
from jax.sharding import PartitionSpec as P

HEAD_WIDTH = 128
MASK_BLOCK_SIZE = 128
BLOCKS_PER_FRAME = 4
FAR_STRIDE = 4
LEVELS = 4


def from_behind(shard, axis, by):
    count = lax.axis_size(axis)
    pairs = [(i, i + by) for i in range(count) if 0 <= i + by < count]
    return lax.ppermute(shard, axis, pairs)


def halo_frame(key_value, key_blocks, frame_rows, seq_count, rep_count, rep_index):
    slab_rows = key_value.shape[1]
    start = jnp.where(rep_index == rep_count - 1, slab_rows - frame_rows, 0)
    payload = lax.dynamic_slice_in_dim(key_value, start, frame_rows, 1)
    key_blocks, payload = lax.optimization_barrier((key_blocks, payload))
    pairs = [(s * rep_count + rep_count - 1, (s + 1) * rep_count) for s in range(seq_count - 1)]
    pairs += [(s * rep_count, (s - 1) * rep_count + rep_count - 1) for s in range(1, seq_count)]
    return lax.ppermute(payload, ("seq", "rep"), pairs), key_blocks


def per_device(query, key_value, key_blocks):
    frame_rows = BLOCKS_PER_FRAME * MASK_BLOCK_SIZE
    query_count = query.shape[0]
    slab_rows = key_value.shape[1]
    columns = key_value.shape[2]
    head_count = columns // HEAD_WIDTH
    slab_blocks = slab_rows // MASK_BLOCK_SIZE
    slab_frames = slab_rows // frame_rows
    far_count = slab_blocks // FAR_STRIDE
    seq_count = lax.axis_size("seq")
    rep_count = lax.axis_size("rep")
    slab_index = lax.axis_index("seq")
    rep_index = lax.axis_index("rep")
    query_frames = query_count // frame_rows
    query_blocks = query_count // MASK_BLOCK_SIZE
    score_scale = 1.0 / math.sqrt(HEAD_WIDTH)
    assert rep_count >= 2 and query_frames * rep_count == slab_frames
    assert far_count % rep_count == 0
    far_share = far_count // rep_count

    halo, key_blocks = halo_frame(key_value, key_blocks, frame_rows, seq_count, rep_count, rep_index)
    halo_valid = ((rep_index == 0) & (slab_index > 0)) | (
        (rep_index == rep_count - 1) & (slab_index < seq_count - 1)
    )
    halo = jnp.where(halo_valid, halo, jnp.zeros_like(halo))

    phases = jnp.maximum(key_blocks[0], 0) % FAR_STRIDE
    stride_grid = key_value.reshape(2, far_count, FAR_STRIDE, MASK_BLOCK_SIZE, columns)
    share_grid = lax.dynamic_slice_in_dim(stride_grid, rep_index * far_share, far_share, 1)
    received = []
    pick_list = []
    valid_list = []
    for tier_index in range(LEVELS):
        distance = 2 ** (tier_index + 1)
        if distance >= seq_count:
            continue
        if seq_count <= 2 * distance:
            ahead = [(q, q + distance) for q in range(seq_count - distance)]
            behind = [(q, q - distance) for q in range(distance, seq_count) if q + distance >= seq_count]
            side = (slab_index + distance >= seq_count).astype(jnp.int32)
            slots = [(ahead + behind, side)]
        else:
            ahead = [(q, q + distance) for q in range(seq_count - distance)]
            behind = [(q, q - distance) for q in range(distance, seq_count)]
            slots = [(ahead, jnp.int32(0)), (behind, jnp.int32(1))]
        for pairs, side in slots:
            slot_index = 2 * tier_index + side
            phase = lax.dynamic_index_in_dim(phases, slot_index, 0, keepdims=False)
            wanted = lax.ppermute(phase[None], "seq", pairs)[0]
            chosen = lax.dynamic_index_in_dim(share_grid, wanted, 2, keepdims=False)
            received.append((chosen, [(b, a) for a, b in pairs]))
            partner = slab_index + (1 - 2 * side) * distance
            inside = (partner >= 0) & (partner < seq_count)
            named = lax.dynamic_index_in_dim(key_blocks, slot_index, 1, keepdims=False)
            pick = (named - partner * slab_blocks - phase) // FAR_STRIDE
            pick_list.append(pick)
            valid_list.append((named >= 0) & inside)
    query, payloads = lax.optimization_barrier((query, [chosen for chosen, _ in received]))
    backs = [back for _, back in received]
    received = [lax.ppermute(chosen[0][None], "seq", back) for chosen, back in zip(payloads, backs)]
    later_values = [chosen[1][None] for chosen in payloads]
    slot_count = len(received)

    near = []
    for head in range(head_count):
        cols = slice(head * HEAD_WIDTH, (head + 1) * HEAD_WIDTH)
        query_head = query[:, cols]
        own_scores = (
            jnp.dot(query_head, key_value[0, :, cols].T, preferred_element_type=jnp.float32)
            * score_scale
        )
        halo_scores = (
            jnp.dot(query_head, halo[0, :, cols].T, preferred_element_type=jnp.float32)
            * score_scale
        )
        halo_scores = jnp.where(halo_valid, halo_scores, -jnp.inf)
        near_top = jnp.maximum(
            jnp.max(own_scores, axis=1, keepdims=True), jnp.max(halo_scores, axis=1, keepdims=True)
        )
        own_exp = jnp.exp(own_scores - near_top)
        halo_exp = jnp.exp(halo_scores - near_top)
        near_total = jnp.sum(own_exp, axis=1, keepdims=True) + jnp.sum(
            halo_exp, axis=1, keepdims=True
        )
        near.append((near_top, own_exp, halo_exp, near_total))
    received, near, later_values = lax.optimization_barrier((received, near, later_values))
    values = [lax.ppermute(chosen, "seq", back) for chosen, back in zip(later_values, backs)]

    def gather_reps(pieces):
        mine = jnp.stack(pieces, 1)
        parts = [mine]
        for k in range(1, rep_count):
            shift = [(r, (r + k) % rep_count) for r in range(rep_count)]
            parts.append(lax.ppermute(mine, "rep", shift))
        return jnp.stack(parts, 2).reshape(slot_count * far_count * MASK_BLOCK_SIZE, columns)

    sources = [(rep_index - k) % rep_count for k in range(rep_count)]
    far_keys = gather_reps(received)
    far_pick = jnp.stack(pick_list, 1)
    far_valid = jnp.stack(valid_list, 1)
    share_ids = jnp.arange(far_share, dtype=jnp.int32)
    candidates = (jnp.stack(sources)[:, None] * far_share + share_ids[None, :]).reshape(far_count)
    far_mask = far_valid[:, :, None] & (far_pick[:, :, None] == candidates[None, None, :])
    far_mask = jnp.repeat(far_mask.reshape(query_blocks, 1, slot_count * far_count), MASK_BLOCK_SIZE, axis=2)

    outputs = []
    for head in range(head_count):
        cols = slice(head * HEAD_WIDTH, (head + 1) * HEAD_WIDTH)
        near_top, own_exp, halo_exp, near_total = near[head]
        far_scores = (
            jnp.dot(query[:, cols], far_keys[:, cols].T, preferred_element_type=jnp.float32)
            * score_scale
        )
        far_scores = jnp.where(
            far_mask, far_scores.reshape(query_blocks, MASK_BLOCK_SIZE, -1), -jnp.inf
        ).reshape(query_count, -1)
        row_top = jnp.maximum(near_top, jnp.max(far_scores, axis=1, keepdims=True))
        near_factor = jnp.exp(near_top - row_top)
        far_exp = jnp.exp(far_scores - row_top)
        row_total = near_total * near_factor + jnp.sum(far_exp, axis=1, keepdims=True)
        near_scale = near_factor / row_total
        own_prob = (own_exp * near_scale).astype(jnp.bfloat16)
        halo_prob = (halo_exp * near_scale).astype(jnp.bfloat16)
        far_prob = (far_exp / row_total).astype(jnp.bfloat16)
        mixed = jnp.dot(own_prob, key_value[1, :, cols], preferred_element_type=jnp.float32)
        mixed = mixed + jnp.dot(halo_prob, halo[1, :, cols], preferred_element_type=jnp.float32)
        outputs.append((mixed, far_prob))
    values, outputs = lax.optimization_barrier((values, outputs))
    far_values = gather_reps(values)
    near_part = jnp.concatenate([mixed for mixed, _ in outputs], axis=1)
    far_part = []
    for head, (_, far_prob) in enumerate(outputs):
        cols = slice(head * HEAD_WIDTH, (head + 1) * HEAD_WIDTH)
        far_part.append(jnp.dot(far_prob, far_values[:, cols], preferred_element_type=jnp.float32))
    return (near_part + jnp.concatenate(far_part, axis=1)).astype(jnp.bfloat16)


def solution(mesh):
    in_specs = (
        P(("grp", "seq", "rep"), "head"),
        P(None, ("grp", "seq"), "head"),
        P(("grp", "seq", "rep"), None),
    )
    out_specs = P(("grp", "seq", "rep"), "head")
    return jax.shard_map(
        per_device, mesh=mesh, in_specs=in_specs, out_specs=out_specs, check_vma=False
    )
```

```python
import math

import jax
import jax.numpy as jnp
from jax import lax
from jax.sharding import PartitionSpec as P

HEAD_WIDTH = 128
MASK_BLOCK_SIZE = 128
BLOCKS_PER_FRAME = 4
FAR_STRIDE = 4
LEVELS = 4


def from_behind(shard, axis, by):
    count = lax.axis_size(axis)
    pairs = [(i, i + by) for i in range(count) if 0 <= i + by < count]
    return lax.ppermute(shard, axis, pairs)


def halo_frame(key_value, key_blocks, frame_rows, seq_count, rep_count, rep_index):
    slab_rows = key_value.shape[1]
    start = jnp.where(rep_index == rep_count - 1, slab_rows - frame_rows, 0)
    payload = lax.dynamic_slice_in_dim(key_value, start, frame_rows, 1)
    key_blocks, payload = lax.optimization_barrier((key_blocks, payload))
    pairs = [(s * rep_count + rep_count - 1, (s + 1) * rep_count) for s in range(seq_count - 1)]
    pairs += [(s * rep_count, (s - 1) * rep_count + rep_count - 1) for s in range(1, seq_count)]
    return lax.ppermute(payload, ("seq", "rep"), pairs), key_blocks


def per_device(query, key_value, key_blocks):
    frame_rows = BLOCKS_PER_FRAME * MASK_BLOCK_SIZE
    query_count = query.shape[0]
    slab_rows = key_value.shape[1]
    columns = key_value.shape[2]
    head_count = columns // HEAD_WIDTH
    slab_blocks = slab_rows // MASK_BLOCK_SIZE
    slab_frames = slab_rows // frame_rows
    far_count = slab_blocks // FAR_STRIDE
    seq_count = lax.axis_size("seq")
    rep_count = lax.axis_size("rep")
    slab_index = lax.axis_index("seq")
    rep_index = lax.axis_index("rep")
    query_frames = query_count // frame_rows
    query_blocks = query_count // MASK_BLOCK_SIZE
    score_scale = 1.0 / math.sqrt(HEAD_WIDTH)
    assert rep_count >= 2 and query_frames * rep_count == slab_frames
    assert far_count % rep_count == 0
    far_share = far_count // rep_count

    halo, key_blocks = halo_frame(key_value, key_blocks, frame_rows, seq_count, rep_count, rep_index)
    halo_valid = ((rep_index == 0) & (slab_index > 0)) | (
        (rep_index == rep_count - 1) & (slab_index < seq_count - 1)
    )
    halo = jnp.where(halo_valid, halo, jnp.zeros_like(halo))

    phases = jnp.maximum(key_blocks[0], 0) % FAR_STRIDE
    stride_grid = key_value.reshape(2, far_count, FAR_STRIDE, MASK_BLOCK_SIZE, columns)
    share_grid = lax.dynamic_slice_in_dim(stride_grid, rep_index * far_share, far_share, 1)
    received = []
    pick_list = []
    valid_list = []
    for tier_index in range(LEVELS):
        distance = 2 ** (tier_index + 1)
        if distance >= seq_count:
            continue
        if seq_count <= 2 * distance:
            ahead = [(q, q + distance) for q in range(seq_count - distance)]
            behind = [(q, q - distance) for q in range(distance, seq_count) if q + distance >= seq_count]
            side = (slab_index + distance >= seq_count).astype(jnp.int32)
            slots = [(ahead + behind, side)]
        else:
            ahead = [(q, q + distance) for q in range(seq_count - distance)]
            behind = [(q, q - distance) for q in range(distance, seq_count)]
            slots = [(ahead, jnp.int32(0)), (behind, jnp.int32(1))]
        for pairs, side in slots:
            slot_index = 2 * tier_index + side
            phase = lax.dynamic_index_in_dim(phases, slot_index, 0, keepdims=False)
            wanted = lax.ppermute(phase[None], "seq", pairs)[0]
            chosen = lax.dynamic_index_in_dim(share_grid, wanted, 2, keepdims=False)
            received.append((chosen, [(b, a) for a, b in pairs]))
            partner = slab_index + (1 - 2 * side) * distance
            inside = (partner >= 0) & (partner < seq_count)
            named = lax.dynamic_index_in_dim(key_blocks, slot_index, 1, keepdims=False)
            pick = (named - partner * slab_blocks - phase) // FAR_STRIDE
            pick_list.append(pick)
            valid_list.append((named >= 0) & inside)
    query, payloads = lax.optimization_barrier((query, [chosen for chosen, _ in received]))
    backs = [back for _, back in received]
    received = [lax.ppermute(chosen[0][None], "seq", back) for chosen, back in zip(payloads, backs)]
    later_values = [chosen[1][None] for chosen in payloads]
    slot_count = len(received)

    near = []
    for head in range(head_count):
        cols = slice(head * HEAD_WIDTH, (head + 1) * HEAD_WIDTH)
        query_head = query[:, cols]
        own_scores = (
            jnp.dot(query_head, key_value[0, :, cols].T, preferred_element_type=jnp.float32)
            * score_scale
        )
        halo_scores = (
            jnp.dot(query_head, halo[0, :, cols].T, preferred_element_type=jnp.float32)
            * score_scale
        )
        halo_scores = jnp.where(halo_valid, halo_scores, -jnp.inf)
        near_top = jnp.maximum(
            jnp.max(own_scores, axis=1, keepdims=True), jnp.max(halo_scores, axis=1, keepdims=True)
        )
        own_exp = jnp.exp(own_scores - near_top)
        halo_exp = jnp.exp(halo_scores - near_top)
        near_total = jnp.sum(own_exp, axis=1, keepdims=True) + jnp.sum(
            halo_exp, axis=1, keepdims=True
        )
        near.append((near_top, own_exp, halo_exp, near_total))
    received, near, later_values = lax.optimization_barrier((received, near, later_values))
    values = [lax.ppermute(chosen, "seq", back) for chosen, back in zip(later_values, backs)]

    def gather_reps(pieces):
        mine = jnp.stack(pieces, 1)
        parts = [mine]
        for k in range(1, rep_count):
            shift = [(r, (r + k) % rep_count) for r in range(rep_count)]
            parts.append(lax.ppermute(mine, "rep", shift))
        return jnp.stack(parts, 2).reshape(slot_count * far_count * MASK_BLOCK_SIZE, columns)

    sources = [(rep_index - k) % rep_count for k in range(rep_count)]
    far_keys = gather_reps(received)
    far_pick = jnp.stack(pick_list, 1)
    far_valid = jnp.stack(valid_list, 1)
    share_ids = jnp.arange(far_share, dtype=jnp.int32)
    candidates = (jnp.stack(sources)[:, None] * far_share + share_ids[None, :]).reshape(far_count)
    far_mask = far_valid[:, :, None] & (far_pick[:, :, None] == candidates[None, None, :])
    far_mask = jnp.repeat(far_mask.reshape(query_blocks, 1, slot_count * far_count), MASK_BLOCK_SIZE, axis=2)

    outputs = []
    for head in range(head_count):
        cols = slice(head * HEAD_WIDTH, (head + 1) * HEAD_WIDTH)
        near_top, own_exp, halo_exp, near_total = near[head]
        far_scores = (
            jnp.dot(query[:, cols], far_keys[:, cols].T, preferred_element_type=jnp.float32)
            * score_scale
        )
        far_scores = jnp.where(
            far_mask, far_scores.reshape(query_blocks, MASK_BLOCK_SIZE, -1), -jnp.inf
        ).reshape(query_count, -1)
        row_top = jnp.maximum(near_top, jnp.max(far_scores, axis=1, keepdims=True))
        near_factor = jnp.exp(near_top - row_top)
        far_exp = jnp.exp(far_scores - row_top)
        row_total = near_total * near_factor + jnp.sum(far_exp, axis=1, keepdims=True)
        near_scale = near_factor / row_total
        own_prob = (own_exp * near_scale).astype(jnp.bfloat16)
        halo_prob = (halo_exp * near_scale).astype(jnp.bfloat16)
        far_prob = (far_exp / row_total).astype(jnp.bfloat16)
        mixed = jnp.dot(own_prob, key_value[1, :, cols], preferred_element_type=jnp.float32)
        mixed = mixed + jnp.dot(halo_prob, halo[1, :, cols], preferred_element_type=jnp.float32)
        outputs.append((mixed, far_prob))
    values, outputs = lax.optimization_barrier((values, outputs))
    far_values = gather_reps(values)
    total = jnp.concatenate([mixed for mixed, _ in outputs], axis=1)
    for head, (_, far_prob) in enumerate(outputs):
        cols = slice(head * HEAD_WIDTH, (head + 1) * HEAD_WIDTH)
        far_part = jnp.dot(far_prob, far_values[:, cols], preferred_element_type=jnp.float32)
        total = total.at[:, cols].add(far_part)
    return total.astype(jnp.bfloat16)


def solution(mesh):
    in_specs = (
        P(("grp", "seq", "rep"), "head"),
        P(None, ("grp", "seq"), "head"),
        P(("grp", "seq", "rep"), None),
    )
    out_specs = P(("grp", "seq", "rep"), "head")
    return jax.shard_map(
        per_device, mesh=mesh, in_specs=in_specs, out_specs=out_specs, check_vma=False
    )
```

```python
import math

import jax
import jax.numpy as jnp
from jax import lax
from jax.sharding import PartitionSpec as P

HEAD_WIDTH = 128
MASK_BLOCK_SIZE = 128
BLOCKS_PER_FRAME = 4
FAR_STRIDE = 4
LEVELS = 4


def from_behind(shard, axis, by):
    count = lax.axis_size(axis)
    pairs = [(i, i + by) for i in range(count) if 0 <= i + by < count]
    return lax.ppermute(shard, axis, pairs)


def halo_frame(key_value, key_blocks, frame_rows, seq_count, rep_count, rep_index):
    slab_rows = key_value.shape[1]
    start = jnp.where(rep_index == rep_count - 1, slab_rows - frame_rows, 0)
    payload = lax.dynamic_slice_in_dim(key_value, start, frame_rows, 1)
    key_blocks, payload = lax.optimization_barrier((key_blocks, payload))
    pairs = [(s * rep_count + rep_count - 1, (s + 1) * rep_count) for s in range(seq_count - 1)]
    pairs += [(s * rep_count, (s - 1) * rep_count + rep_count - 1) for s in range(1, seq_count)]
    return lax.ppermute(payload[0], ("seq", "rep"), pairs), payload[1], pairs, key_blocks


def per_device(query, key_value, key_blocks):
    frame_rows = BLOCKS_PER_FRAME * MASK_BLOCK_SIZE
    query_count = query.shape[0]
    slab_rows = key_value.shape[1]
    columns = key_value.shape[2]
    head_count = columns // HEAD_WIDTH
    slab_blocks = slab_rows // MASK_BLOCK_SIZE
    slab_frames = slab_rows // frame_rows
    far_count = slab_blocks // FAR_STRIDE
    seq_count = lax.axis_size("seq")
    rep_count = lax.axis_size("rep")
    slab_index = lax.axis_index("seq")
    rep_index = lax.axis_index("rep")
    query_frames = query_count // frame_rows
    query_blocks = query_count // MASK_BLOCK_SIZE
    score_scale = 1.0 / math.sqrt(HEAD_WIDTH)
    assert rep_count >= 2 and query_frames * rep_count == slab_frames
    assert far_count % rep_count == 0
    far_share = far_count // rep_count

    halo_keys, halo_value_payload, halo_pairs, key_blocks = halo_frame(
        key_value, key_blocks, frame_rows, seq_count, rep_count, rep_index
    )
    halo_valid = ((rep_index == 0) & (slab_index > 0)) | (
        (rep_index == rep_count - 1) & (slab_index < seq_count - 1)
    )
    halo_keys = jnp.where(halo_valid, halo_keys, jnp.zeros_like(halo_keys))

    phases = jnp.maximum(key_blocks[0], 0) % FAR_STRIDE
    stride_grid = key_value.reshape(2, far_count, FAR_STRIDE, MASK_BLOCK_SIZE, columns)
    share_grid = lax.dynamic_slice_in_dim(stride_grid, rep_index * far_share, far_share, 1)
    received = []
    pick_list = []
    valid_list = []
    for tier_index in range(LEVELS):
        distance = 2 ** (tier_index + 1)
        if distance >= seq_count:
            continue
        if seq_count <= 2 * distance:
            ahead = [(q, q + distance) for q in range(seq_count - distance)]
            behind = [(q, q - distance) for q in range(distance, seq_count) if q + distance >= seq_count]
            side = (slab_index + distance >= seq_count).astype(jnp.int32)
            slots = [(ahead + behind, side)]
        else:
            ahead = [(q, q + distance) for q in range(seq_count - distance)]
            behind = [(q, q - distance) for q in range(distance, seq_count)]
            slots = [(ahead, jnp.int32(0)), (behind, jnp.int32(1))]
        for pairs, side in slots:
            slot_index = 2 * tier_index + side
            phase = lax.dynamic_index_in_dim(phases, slot_index, 0, keepdims=False)
            wanted = lax.ppermute(phase[None], "seq", pairs)[0]
            chosen = lax.dynamic_index_in_dim(share_grid, wanted, 2, keepdims=False)
            received.append((chosen, [(b, a) for a, b in pairs]))
            partner = slab_index + (1 - 2 * side) * distance
            inside = (partner >= 0) & (partner < seq_count)
            named = lax.dynamic_index_in_dim(key_blocks, slot_index, 1, keepdims=False)
            pick = (named - partner * slab_blocks - phase) // FAR_STRIDE
            pick_list.append(pick)
            valid_list.append((named >= 0) & inside)
    query, payloads = lax.optimization_barrier((query, [chosen for chosen, _ in received]))
    backs = [back for _, back in received]
    received = [lax.ppermute(chosen[0][None], "seq", back) for chosen, back in zip(payloads, backs)]
    later_values = [chosen[1][None] for chosen in payloads]
    slot_count = len(received)

    near = []
    for head in range(head_count):
        cols = slice(head * HEAD_WIDTH, (head + 1) * HEAD_WIDTH)
        query_head = query[:, cols]
        own_scores = (
            jnp.dot(query_head, key_value[0, :, cols].T, preferred_element_type=jnp.float32)
            * score_scale
        )
        halo_scores = (
            jnp.dot(query_head, halo_keys[:, cols].T, preferred_element_type=jnp.float32)
            * score_scale
        )
        halo_scores = jnp.where(halo_valid, halo_scores, -jnp.inf)
        near_top = jnp.maximum(
            jnp.max(own_scores, axis=1, keepdims=True), jnp.max(halo_scores, axis=1, keepdims=True)
        )
        own_exp = jnp.exp(own_scores - near_top)
        halo_exp = jnp.exp(halo_scores - near_top)
        near_total = jnp.sum(own_exp, axis=1, keepdims=True) + jnp.sum(
            halo_exp, axis=1, keepdims=True
        )
        near.append((near_top, own_exp, halo_exp, near_total))
    received, near, later_values, halo_value_payload = lax.optimization_barrier(
        (received, near, later_values, halo_value_payload)
    )
    values = [lax.ppermute(chosen, "seq", back) for chosen, back in zip(later_values, backs)]
    halo_values = lax.ppermute(halo_value_payload, ("seq", "rep"), halo_pairs)

    def gather_reps(pieces):
        mine = jnp.stack(pieces, 1)
        parts = [mine]
        for k in range(1, rep_count):
            shift = [(r, (r + k) % rep_count) for r in range(rep_count)]
            parts.append(lax.ppermute(mine, "rep", shift))
        return jnp.stack(parts, 2).reshape(slot_count * far_count * MASK_BLOCK_SIZE, columns)

    sources = [(rep_index - k) % rep_count for k in range(rep_count)]
    far_keys = gather_reps(received)
    far_pick = jnp.stack(pick_list, 1)
    far_valid = jnp.stack(valid_list, 1)
    share_ids = jnp.arange(far_share, dtype=jnp.int32)
    candidates = (jnp.stack(sources)[:, None] * far_share + share_ids[None, :]).reshape(far_count)
    far_mask = far_valid[:, :, None] & (far_pick[:, :, None] == candidates[None, None, :])
    far_mask = jnp.repeat(far_mask.reshape(query_blocks, 1, slot_count * far_count), MASK_BLOCK_SIZE, axis=2)

    outputs = []
    for head in range(head_count):
        cols = slice(head * HEAD_WIDTH, (head + 1) * HEAD_WIDTH)
        near_top, own_exp, halo_exp, near_total = near[head]
        far_scores = (
            jnp.dot(query[:, cols], far_keys[:, cols].T, preferred_element_type=jnp.float32)
            * score_scale
        )
        far_scores = jnp.where(
            far_mask, far_scores.reshape(query_blocks, MASK_BLOCK_SIZE, -1), -jnp.inf
        ).reshape(query_count, -1)
        row_top = jnp.maximum(near_top, jnp.max(far_scores, axis=1, keepdims=True))
        near_factor = jnp.exp(near_top - row_top)
        far_exp = jnp.exp(far_scores - row_top)
        row_total = near_total * near_factor + jnp.sum(far_exp, axis=1, keepdims=True)
        near_scale = near_factor / row_total
        own_prob = (own_exp * near_scale).astype(jnp.bfloat16)
        halo_prob = (halo_exp * near_scale).astype(jnp.bfloat16)
        far_prob = (far_exp / row_total).astype(jnp.bfloat16)
        mixed = jnp.dot(own_prob, key_value[1, :, cols], preferred_element_type=jnp.float32)
        outputs.append((mixed, far_prob, halo_prob))
    values, halo_values, outputs = lax.optimization_barrier((values, halo_values, outputs))
    halo_values = jnp.where(halo_valid, halo_values, jnp.zeros_like(halo_values))
    outputs = [
        (mixed + jnp.dot(halo_prob, halo_values[:, head * HEAD_WIDTH : (head + 1) * HEAD_WIDTH],
                         preferred_element_type=jnp.float32), far_prob)
        for head, (mixed, far_prob, halo_prob) in enumerate(outputs)
    ]
    far_values = gather_reps(values)
    near_part = jnp.concatenate([mixed for mixed, _ in outputs], axis=1)
    far_part = []
    for head, (_, far_prob) in enumerate(outputs):
        cols = slice(head * HEAD_WIDTH, (head + 1) * HEAD_WIDTH)
        far_part.append(jnp.dot(far_prob, far_values[:, cols], preferred_element_type=jnp.float32))
    return (near_part + jnp.concatenate(far_part, axis=1)).astype(jnp.bfloat16)


def solution(mesh):
    in_specs = (
        P(("grp", "seq", "rep"), "head"),
        P(None, ("grp", "seq"), "head"),
        P(("grp", "seq", "rep"), None),
    )
    out_specs = P(("grp", "seq", "rep"), "head")
    return jax.shard_map(
        per_device, mesh=mesh, in_specs=in_specs, out_specs=out_specs, check_vma=False
    )
```

```python
import math

import jax
import jax.numpy as jnp
from jax import lax
from jax.sharding import PartitionSpec as P

HEAD_WIDTH = 128
MASK_BLOCK_SIZE = 128
BLOCKS_PER_FRAME = 4
FAR_STRIDE = 4
LEVELS = 4


def from_behind(shard, axis, by):
    count = lax.axis_size(axis)
    pairs = [(i, i + by) for i in range(count) if 0 <= i + by < count]
    return lax.ppermute(shard, axis, pairs)


def halo_frame(key_value, key_blocks, frame_rows, seq_count, rep_count, rep_index):
    slab_rows = key_value.shape[1]
    last = lax.slice_in_dim(key_value, slab_rows - frame_rows, slab_rows, axis=1)
    first = lax.slice_in_dim(key_value, 0, frame_rows, axis=1)
    payload = jnp.where(rep_index == rep_count - 1, last, first)
    key_blocks, payload = lax.optimization_barrier((key_blocks, payload))
    pairs = [(s * rep_count + rep_count - 1, (s + 1) * rep_count) for s in range(seq_count - 1)]
    pairs += [(s * rep_count, (s - 1) * rep_count + rep_count - 1) for s in range(1, seq_count)]
    return lax.ppermute(payload, ("seq", "rep"), pairs), key_blocks


def per_device(query, key_value, key_blocks):
    frame_rows = BLOCKS_PER_FRAME * MASK_BLOCK_SIZE
    query_count = query.shape[0]
    slab_rows = key_value.shape[1]
    columns = key_value.shape[2]
    head_count = columns // HEAD_WIDTH
    slab_blocks = slab_rows // MASK_BLOCK_SIZE
    slab_frames = slab_rows // frame_rows
    far_count = slab_blocks // FAR_STRIDE
    seq_count = lax.axis_size("seq")
    rep_count = lax.axis_size("rep")
    slab_index = lax.axis_index("seq")
    rep_index = lax.axis_index("rep")
    query_frames = query_count // frame_rows
    query_blocks = query_count // MASK_BLOCK_SIZE
    score_scale = 1.0 / math.sqrt(HEAD_WIDTH)
    assert rep_count >= 2 and query_frames * rep_count == slab_frames
    assert far_count % rep_count == 0
    far_share = far_count // rep_count

    halo, key_blocks = halo_frame(key_value, key_blocks, frame_rows, seq_count, rep_count, rep_index)
    halo_valid = ((rep_index == 0) & (slab_index > 0)) | (
        (rep_index == rep_count - 1) & (slab_index < seq_count - 1)
    )
    halo = jnp.where(halo_valid, halo, jnp.zeros_like(halo))

    phases = jnp.maximum(key_blocks[0], 0) % FAR_STRIDE
    stride_grid = key_value.reshape(2, far_count, FAR_STRIDE, MASK_BLOCK_SIZE, columns)
    share_grid = lax.dynamic_slice_in_dim(stride_grid, rep_index * far_share, far_share, 1)
    received = []
    pick_list = []
    valid_list = []
    for tier_index in range(LEVELS):
        distance = 2 ** (tier_index + 1)
        if distance >= seq_count:
            continue
        if seq_count <= 2 * distance:
            ahead = [(q, q + distance) for q in range(seq_count - distance)]
            behind = [(q, q - distance) for q in range(distance, seq_count) if q + distance >= seq_count]
            side = (slab_index + distance >= seq_count).astype(jnp.int32)
            slots = [(ahead + behind, side)]
        else:
            ahead = [(q, q + distance) for q in range(seq_count - distance)]
            behind = [(q, q - distance) for q in range(distance, seq_count)]
            slots = [(ahead, jnp.int32(0)), (behind, jnp.int32(1))]
        for pairs, side in slots:
            slot_index = 2 * tier_index + side
            phase = lax.dynamic_index_in_dim(phases, slot_index, 0, keepdims=False)
            wanted = lax.ppermute(phase[None], "seq", pairs)[0]
            chosen = lax.dynamic_index_in_dim(share_grid, wanted, 2, keepdims=False)
            received.append((chosen, [(b, a) for a, b in pairs]))
            partner = slab_index + (1 - 2 * side) * distance
            inside = (partner >= 0) & (partner < seq_count)
            named = lax.dynamic_index_in_dim(key_blocks, slot_index, 1, keepdims=False)
            pick = (named - partner * slab_blocks - phase) // FAR_STRIDE
            pick_list.append(pick)
            valid_list.append((named >= 0) & inside)
    query, payloads = lax.optimization_barrier((query, [chosen for chosen, _ in received]))
    backs = [back for _, back in received]
    received = [lax.ppermute(chosen[0][None], "seq", back) for chosen, back in zip(payloads, backs)]
    later_values = [chosen[1][None] for chosen in payloads]
    slot_count = len(received)

    near = []
    for head in range(head_count):
        cols = slice(head * HEAD_WIDTH, (head + 1) * HEAD_WIDTH)
        query_head = query[:, cols]
        own_scores = (
            jnp.dot(query_head, key_value[0, :, cols].T, preferred_element_type=jnp.float32)
            * score_scale
        )
        halo_scores = (
            jnp.dot(query_head, halo[0, :, cols].T, preferred_element_type=jnp.float32)
            * score_scale
        )
        halo_scores = jnp.where(halo_valid, halo_scores, -jnp.inf)
        near_top = jnp.maximum(
            jnp.max(own_scores, axis=1, keepdims=True), jnp.max(halo_scores, axis=1, keepdims=True)
        )
        own_exp = jnp.exp(own_scores - near_top)
        halo_exp = jnp.exp(halo_scores - near_top)
        near_total = jnp.sum(own_exp, axis=1, keepdims=True) + jnp.sum(
            halo_exp, axis=1, keepdims=True
        )
        near.append((near_top, own_exp, halo_exp, near_total))
    received, near, later_values = lax.optimization_barrier((received, near, later_values))
    values = [lax.ppermute(chosen, "seq", back) for chosen, back in zip(later_values, backs)]

    def gather_reps(pieces):
        mine = jnp.stack(pieces, 1)
        parts = [mine]
        for k in range(1, rep_count):
            shift = [(r, (r + k) % rep_count) for r in range(rep_count)]
            parts.append(lax.ppermute(mine, "rep", shift))
        return jnp.stack(parts, 2).reshape(slot_count * far_count * MASK_BLOCK_SIZE, columns)

    sources = [(rep_index - k) % rep_count for k in range(rep_count)]
    far_keys = gather_reps(received)
    far_pick = jnp.stack(pick_list, 1)
    far_valid = jnp.stack(valid_list, 1)
    share_ids = jnp.arange(far_share, dtype=jnp.int32)
    candidates = (jnp.stack(sources)[:, None] * far_share + share_ids[None, :]).reshape(far_count)
    far_mask = far_valid[:, :, None] & (far_pick[:, :, None] == candidates[None, None, :])
    far_mask = jnp.repeat(far_mask.reshape(query_blocks, 1, slot_count * far_count), MASK_BLOCK_SIZE, axis=2)

    outputs = []
    for head in range(head_count):
        cols = slice(head * HEAD_WIDTH, (head + 1) * HEAD_WIDTH)
        near_top, own_exp, halo_exp, near_total = near[head]
        far_scores = (
            jnp.dot(query[:, cols], far_keys[:, cols].T, preferred_element_type=jnp.float32)
            * score_scale
        )
        far_scores = jnp.where(
            far_mask, far_scores.reshape(query_blocks, MASK_BLOCK_SIZE, -1), -jnp.inf
        ).reshape(query_count, -1)
        row_top = jnp.maximum(near_top, jnp.max(far_scores, axis=1, keepdims=True))
        near_factor = jnp.exp(near_top - row_top)
        far_exp = jnp.exp(far_scores - row_top)
        row_total = near_total * near_factor + jnp.sum(far_exp, axis=1, keepdims=True)
        near_scale = near_factor / row_total
        own_prob = (own_exp * near_scale).astype(jnp.bfloat16)
        halo_prob = (halo_exp * near_scale).astype(jnp.bfloat16)
        far_prob = (far_exp / row_total).astype(jnp.bfloat16)
        mixed = jnp.dot(own_prob, key_value[1, :, cols], preferred_element_type=jnp.float32)
        mixed = mixed + jnp.dot(halo_prob, halo[1, :, cols], preferred_element_type=jnp.float32)
        outputs.append((mixed, far_prob))
    values, outputs = lax.optimization_barrier((values, outputs))
    far_values = gather_reps(values)
    near_part = jnp.concatenate([mixed for mixed, _ in outputs], axis=1)
    far_part = []
    for head, (_, far_prob) in enumerate(outputs):
        cols = slice(head * HEAD_WIDTH, (head + 1) * HEAD_WIDTH)
        far_part.append(jnp.dot(far_prob, far_values[:, cols], preferred_element_type=jnp.float32))
    return (near_part + jnp.concatenate(far_part, axis=1)).astype(jnp.bfloat16)


def solution(mesh):
    in_specs = (
        P(("grp", "seq", "rep"), "head"),
        P(None, ("grp", "seq"), "head"),
        P(("grp", "seq", "rep"), None),
    )
    out_specs = P(("grp", "seq", "rep"), "head")
    return jax.shard_map(
        per_device, mesh=mesh, in_specs=in_specs, out_specs=out_specs, check_vma=False
    )
```

```python
import math

import jax
import jax.numpy as jnp
from jax import lax
from jax.sharding import PartitionSpec as P

HEAD_WIDTH = 128
MASK_BLOCK_SIZE = 128
BLOCKS_PER_FRAME = 4
FAR_STRIDE = 4
LEVELS = 4


def from_behind(shard, axis, by):
    count = lax.axis_size(axis)
    pairs = [(i, i + by) for i in range(count) if 0 <= i + by < count]
    return lax.ppermute(shard, axis, pairs)


def halo_frame(key_value, key_blocks, frame_rows, seq_count, rep_count, rep_index):
    slab_rows = key_value.shape[1]
    last = lax.slice_in_dim(key_value, slab_rows - frame_rows, slab_rows, axis=1)
    first = lax.slice_in_dim(key_value, 0, frame_rows, axis=1)
    payload = jnp.where(rep_index == rep_count - 1, last, first)
    payload = lax.optimization_barrier(payload)
    key_blocks = key_blocks + jnp.sum(jnp.isnan(payload), dtype=jnp.int32)
    pairs = [(s * rep_count + rep_count - 1, (s + 1) * rep_count) for s in range(seq_count - 1)]
    pairs += [(s * rep_count, (s - 1) * rep_count + rep_count - 1) for s in range(1, seq_count)]
    return lax.ppermute(payload, ("seq", "rep"), pairs), key_blocks


def per_device(query, key_value, key_blocks):
    frame_rows = BLOCKS_PER_FRAME * MASK_BLOCK_SIZE
    query_count = query.shape[0]
    slab_rows = key_value.shape[1]
    columns = key_value.shape[2]
    head_count = columns // HEAD_WIDTH
    slab_blocks = slab_rows // MASK_BLOCK_SIZE
    slab_frames = slab_rows // frame_rows
    far_count = slab_blocks // FAR_STRIDE
    seq_count = lax.axis_size("seq")
    rep_count = lax.axis_size("rep")
    slab_index = lax.axis_index("seq")
    rep_index = lax.axis_index("rep")
    query_frames = query_count // frame_rows
    query_blocks = query_count // MASK_BLOCK_SIZE
    score_scale = 1.0 / math.sqrt(HEAD_WIDTH)
    assert rep_count >= 2 and query_frames * rep_count == slab_frames
    assert far_count % rep_count == 0
    far_share = far_count // rep_count

    halo, key_blocks = halo_frame(key_value, key_blocks, frame_rows, seq_count, rep_count, rep_index)
    halo_valid = ((rep_index == 0) & (slab_index > 0)) | (
        (rep_index == rep_count - 1) & (slab_index < seq_count - 1)
    )
    halo = jnp.where(halo_valid, halo, jnp.zeros_like(halo))

    phases = jnp.maximum(key_blocks[0], 0) % FAR_STRIDE
    stride_grid = key_value.reshape(2, far_count, FAR_STRIDE, MASK_BLOCK_SIZE, columns)
    share_grid = lax.dynamic_slice_in_dim(stride_grid, rep_index * far_share, far_share, 1)
    received = []
    pick_list = []
    valid_list = []
    for tier_index in range(LEVELS):
        distance = 2 ** (tier_index + 1)
        if distance >= seq_count:
            continue
        if seq_count <= 2 * distance:
            ahead = [(q, q + distance) for q in range(seq_count - distance)]
            behind = [(q, q - distance) for q in range(distance, seq_count) if q + distance >= seq_count]
            side = (slab_index + distance >= seq_count).astype(jnp.int32)
            slots = [(ahead + behind, side)]
        else:
            ahead = [(q, q + distance) for q in range(seq_count - distance)]
            behind = [(q, q - distance) for q in range(distance, seq_count)]
            slots = [(ahead, jnp.int32(0)), (behind, jnp.int32(1))]
        for pairs, side in slots:
            slot_index = 2 * tier_index + side
            phase = lax.dynamic_index_in_dim(phases, slot_index, 0, keepdims=False)
            wanted = lax.ppermute(phase[None], "seq", pairs)[0]
            chosen = lax.dynamic_index_in_dim(share_grid, wanted, 2, keepdims=False)
            received.append((chosen, [(b, a) for a, b in pairs]))
            partner = slab_index + (1 - 2 * side) * distance
            inside = (partner >= 0) & (partner < seq_count)
            named = lax.dynamic_index_in_dim(key_blocks, slot_index, 1, keepdims=False)
            pick = (named - partner * slab_blocks - phase) // FAR_STRIDE
            pick_list.append(pick)
            valid_list.append((named >= 0) & inside)
    query, payloads = lax.optimization_barrier((query, [chosen for chosen, _ in received]))
    backs = [back for _, back in received]
    received = [lax.ppermute(chosen[0][None], "seq", back) for chosen, back in zip(payloads, backs)]
    later_values = [chosen[1][None] for chosen in payloads]
    slot_count = len(received)

    near = []
    for head in range(head_count):
        cols = slice(head * HEAD_WIDTH, (head + 1) * HEAD_WIDTH)
        query_head = query[:, cols]
        own_scores = (
            jnp.dot(query_head, key_value[0, :, cols].T, preferred_element_type=jnp.float32)
            * score_scale
        )
        halo_scores = (
            jnp.dot(query_head, halo[0, :, cols].T, preferred_element_type=jnp.float32)
            * score_scale
        )
        halo_scores = jnp.where(halo_valid, halo_scores, -jnp.inf)
        near_top = jnp.maximum(
            jnp.max(own_scores, axis=1, keepdims=True), jnp.max(halo_scores, axis=1, keepdims=True)
        )
        own_exp = jnp.exp(own_scores - near_top)
        halo_exp = jnp.exp(halo_scores - near_top)
        near_total = jnp.sum(own_exp, axis=1, keepdims=True) + jnp.sum(
            halo_exp, axis=1, keepdims=True
        )
        near.append((near_top, own_exp, halo_exp, near_total))
    received, near, later_values = lax.optimization_barrier((received, near, later_values))
    values = [lax.ppermute(chosen, "seq", back) for chosen, back in zip(later_values, backs)]

    def gather_reps(pieces):
        mine = jnp.stack(pieces, 1)
        parts = [mine]
        for k in range(1, rep_count):
            shift = [(r, (r + k) % rep_count) for r in range(rep_count)]
            parts.append(lax.ppermute(mine, "rep", shift))
        return jnp.stack(parts, 2).reshape(slot_count * far_count * MASK_BLOCK_SIZE, columns)

    sources = [(rep_index - k) % rep_count for k in range(rep_count)]
    far_keys = gather_reps(received)
    far_pick = jnp.stack(pick_list, 1)
    far_valid = jnp.stack(valid_list, 1)
    share_ids = jnp.arange(far_share, dtype=jnp.int32)
    candidates = (jnp.stack(sources)[:, None] * far_share + share_ids[None, :]).reshape(far_count)
    far_mask = far_valid[:, :, None] & (far_pick[:, :, None] == candidates[None, None, :])
    far_mask = jnp.repeat(far_mask.reshape(query_blocks, 1, slot_count * far_count), MASK_BLOCK_SIZE, axis=2)

    outputs = []
    for head in range(head_count):
        cols = slice(head * HEAD_WIDTH, (head + 1) * HEAD_WIDTH)
        near_top, own_exp, halo_exp, near_total = near[head]
        far_scores = (
            jnp.dot(query[:, cols], far_keys[:, cols].T, preferred_element_type=jnp.float32)
            * score_scale
        )
        far_scores = jnp.where(
            far_mask, far_scores.reshape(query_blocks, MASK_BLOCK_SIZE, -1), -jnp.inf
        ).reshape(query_count, -1)
        row_top = jnp.maximum(near_top, jnp.max(far_scores, axis=1, keepdims=True))
        near_factor = jnp.exp(near_top - row_top)
        far_exp = jnp.exp(far_scores - row_top)
        row_total = near_total * near_factor + jnp.sum(far_exp, axis=1, keepdims=True)
        near_scale = near_factor / row_total
        own_prob = (own_exp * near_scale).astype(jnp.bfloat16)
        halo_prob = (halo_exp * near_scale).astype(jnp.bfloat16)
        far_prob = (far_exp / row_total).astype(jnp.bfloat16)
        mixed = jnp.dot(own_prob, key_value[1, :, cols], preferred_element_type=jnp.float32)
        mixed = mixed + jnp.dot(halo_prob, halo[1, :, cols], preferred_element_type=jnp.float32)
        outputs.append((mixed, far_prob))
    values, outputs = lax.optimization_barrier((values, outputs))
    far_values = gather_reps(values)
    near_part = jnp.concatenate([mixed for mixed, _ in outputs], axis=1)
    far_part = []
    for head, (_, far_prob) in enumerate(outputs):
        cols = slice(head * HEAD_WIDTH, (head + 1) * HEAD_WIDTH)
        far_part.append(jnp.dot(far_prob, far_values[:, cols], preferred_element_type=jnp.float32))
    return (near_part + jnp.concatenate(far_part, axis=1)).astype(jnp.bfloat16)


def solution(mesh):
    in_specs = (
        P(("grp", "seq", "rep"), "head"),
        P(None, ("grp", "seq"), "head"),
        P(("grp", "seq", "rep"), None),
    )
    out_specs = P(("grp", "seq", "rep"), "head")
    return jax.shard_map(
        per_device, mesh=mesh, in_specs=in_specs, out_specs=out_specs, check_vma=False
    )
```

```python
import math

import jax
import jax.numpy as jnp
from jax import lax
from jax.sharding import PartitionSpec as P

HEAD_WIDTH = 128
MASK_BLOCK_SIZE = 128
BLOCKS_PER_FRAME = 4
FAR_STRIDE = 4
LEVELS = 4


def from_behind(shard, axis, by):
    count = lax.axis_size(axis)
    pairs = [(i, i + by) for i in range(count) if 0 <= i + by < count]
    return lax.ppermute(shard, axis, pairs)


def halo_frame(key_value, key_blocks, frame_rows, seq_count, rep_count, rep_index):
    slab_rows = key_value.shape[1]
    last = lax.slice_in_dim(key_value, slab_rows - frame_rows, slab_rows, axis=1)
    first = lax.slice_in_dim(key_value, 0, frame_rows, axis=1)
    payload = jnp.where(rep_index == rep_count - 1, last, first)
    pairs = [(s * rep_count + rep_count - 1, (s + 1) * rep_count) for s in range(seq_count - 1)]
    pairs += [(s * rep_count, (s - 1) * rep_count + rep_count - 1) for s in range(1, seq_count)]
    return lax.ppermute(payload, ("seq", "rep"), pairs), key_blocks


def per_device(query, key_value, key_blocks):
    frame_rows = BLOCKS_PER_FRAME * MASK_BLOCK_SIZE
    query_count = query.shape[0]
    slab_rows = key_value.shape[1]
    columns = key_value.shape[2]
    head_count = columns // HEAD_WIDTH
    slab_blocks = slab_rows // MASK_BLOCK_SIZE
    slab_frames = slab_rows // frame_rows
    far_count = slab_blocks // FAR_STRIDE
    seq_count = lax.axis_size("seq")
    rep_count = lax.axis_size("rep")
    slab_index = lax.axis_index("seq")
    rep_index = lax.axis_index("rep")
    query_frames = query_count // frame_rows
    query_blocks = query_count // MASK_BLOCK_SIZE
    score_scale = 1.0 / math.sqrt(HEAD_WIDTH)
    assert rep_count >= 2 and query_frames * rep_count == slab_frames
    assert far_count % rep_count == 0
    far_share = far_count // rep_count

    halo, key_blocks = halo_frame(key_value, key_blocks, frame_rows, seq_count, rep_count, rep_index)
    halo_valid = ((rep_index == 0) & (slab_index > 0)) | (
        (rep_index == rep_count - 1) & (slab_index < seq_count - 1)
    )
    halo = jnp.where(halo_valid, halo, jnp.zeros_like(halo))

    phases = jnp.maximum(key_blocks[0], 0) % FAR_STRIDE
    stride_grid = key_value.reshape(2, far_count, FAR_STRIDE, MASK_BLOCK_SIZE, columns)
    share_grid = lax.dynamic_slice_in_dim(stride_grid, rep_index * far_share, far_share, 1)
    received = []
    pick_list = []
    valid_list = []
    for tier_index in range(LEVELS):
        distance = 2 ** (tier_index + 1)
        if distance >= seq_count:
            continue
        if seq_count <= 2 * distance:
            ahead = [(q, q + distance) for q in range(seq_count - distance)]
            behind = [(q, q - distance) for q in range(distance, seq_count) if q + distance >= seq_count]
            side = (slab_index + distance >= seq_count).astype(jnp.int32)
            slots = [(ahead + behind, side)]
        else:
            ahead = [(q, q + distance) for q in range(seq_count - distance)]
            behind = [(q, q - distance) for q in range(distance, seq_count)]
            slots = [(ahead, jnp.int32(0)), (behind, jnp.int32(1))]
        for pairs, side in slots:
            slot_index = 2 * tier_index + side
            phase = lax.dynamic_index_in_dim(phases, slot_index, 0, keepdims=False)
            wanted = lax.ppermute(phase[None], "seq", pairs)[0]
            chosen = lax.dynamic_index_in_dim(share_grid, wanted, 2, keepdims=False)
            received.append((chosen, [(b, a) for a, b in pairs]))
            partner = slab_index + (1 - 2 * side) * distance
            inside = (partner >= 0) & (partner < seq_count)
            named = lax.dynamic_index_in_dim(key_blocks, slot_index, 1, keepdims=False)
            pick = (named - partner * slab_blocks - phase) // FAR_STRIDE
            pick_list.append(pick)
            valid_list.append((named >= 0) & inside)
    query, payloads = lax.optimization_barrier((query, [chosen for chosen, _ in received]))
    backs = [back for _, back in received]
    received = [lax.ppermute(chosen[0][None], "seq", back) for chosen, back in zip(payloads, backs)]
    later_values = [chosen[1][None] for chosen in payloads]
    slot_count = len(received)

    near = []
    for head in range(head_count):
        cols = slice(head * HEAD_WIDTH, (head + 1) * HEAD_WIDTH)
        query_head = query[:, cols]
        own_scores = (
            jnp.dot(query_head, key_value[0, :, cols].T, preferred_element_type=jnp.float32)
            * score_scale
        )
        halo_scores = (
            jnp.dot(query_head, halo[0, :, cols].T, preferred_element_type=jnp.float32)
            * score_scale
        )
        halo_scores = jnp.where(halo_valid, halo_scores, -jnp.inf)
        near_top = jnp.maximum(
            jnp.max(own_scores, axis=1, keepdims=True), jnp.max(halo_scores, axis=1, keepdims=True)
        )
        own_exp = jnp.exp(own_scores - near_top)
        halo_exp = jnp.exp(halo_scores - near_top)
        near_total = jnp.sum(own_exp, axis=1, keepdims=True) + jnp.sum(
            halo_exp, axis=1, keepdims=True
        )
        near.append((near_top, own_exp, halo_exp, near_total))
    received, near, later_values = lax.optimization_barrier((received, near, later_values))
    values = [lax.ppermute(chosen, "seq", back) for chosen, back in zip(later_values, backs)]

    def gather_reps(pieces):
        mine = jnp.stack(pieces, 1)
        parts = [mine]
        for k in range(1, rep_count):
            shift = [(r, (r + k) % rep_count) for r in range(rep_count)]
            parts.append(lax.ppermute(mine, "rep", shift))
        return jnp.stack(parts, 2).reshape(slot_count * far_count * MASK_BLOCK_SIZE, columns)

    sources = [(rep_index - k) % rep_count for k in range(rep_count)]
    far_keys = gather_reps(received)
    far_pick = jnp.stack(pick_list, 1)
    far_valid = jnp.stack(valid_list, 1)
    share_ids = jnp.arange(far_share, dtype=jnp.int32)
    candidates = (jnp.stack(sources)[:, None] * far_share + share_ids[None, :]).reshape(far_count)
    far_mask = far_valid[:, :, None] & (far_pick[:, :, None] == candidates[None, None, :])
    far_mask = jnp.repeat(far_mask.reshape(query_blocks, 1, slot_count * far_count), MASK_BLOCK_SIZE, axis=2)

    outputs = []
    for head in range(head_count):
        cols = slice(head * HEAD_WIDTH, (head + 1) * HEAD_WIDTH)
        near_top, own_exp, halo_exp, near_total = near[head]
        far_scores = (
            jnp.dot(query[:, cols], far_keys[:, cols].T, preferred_element_type=jnp.float32)
            * score_scale
        )
        far_scores = jnp.where(
            far_mask, far_scores.reshape(query_blocks, MASK_BLOCK_SIZE, -1), -jnp.inf
        ).reshape(query_count, -1)
        row_top = jnp.maximum(near_top, jnp.max(far_scores, axis=1, keepdims=True))
        near_factor = jnp.exp(near_top - row_top)
        far_exp = jnp.exp(far_scores - row_top)
        row_total = near_total * near_factor + jnp.sum(far_exp, axis=1, keepdims=True)
        near_scale = near_factor / row_total
        own_prob = (own_exp * near_scale).astype(jnp.bfloat16)
        halo_prob = (halo_exp * near_scale).astype(jnp.bfloat16)
        far_prob = (far_exp / row_total).astype(jnp.bfloat16)
        mixed = jnp.dot(own_prob, key_value[1, :, cols], preferred_element_type=jnp.float32)
        mixed = mixed + jnp.dot(halo_prob, halo[1, :, cols], preferred_element_type=jnp.float32)
        outputs.append((mixed, far_prob))
    values, outputs = lax.optimization_barrier((values, outputs))
    far_values = gather_reps(values)
    near_part = jnp.concatenate([mixed for mixed, _ in outputs], axis=1)
    far_part = []
    for head, (_, far_prob) in enumerate(outputs):
        cols = slice(head * HEAD_WIDTH, (head + 1) * HEAD_WIDTH)
        far_part.append(jnp.dot(far_prob, far_values[:, cols], preferred_element_type=jnp.float32))
    return (near_part + jnp.concatenate(far_part, axis=1)).astype(jnp.bfloat16)


def solution(mesh):
    in_specs = (
        P(("grp", "seq", "rep"), "head"),
        P(None, ("grp", "seq"), "head"),
        P(("grp", "seq", "rep"), None),
    )
    out_specs = P(("grp", "seq", "rep"), "head")
    return jax.shard_map(
        per_device, mesh=mesh, in_specs=in_specs, out_specs=out_specs, check_vma=False
    )
```
